32 devices in a mesh: freq: 4 (over x, core), tile: 8 (over z, y).
Axes of the slice: x: 2, y: 2, z: 4, core: 2. Of those that a mesh axis runs over, the one named last changes fastest.
Arguments:
- travel_time: float32 [512, 8, 512], P('tile', None, 'freq'), may hold values from 0 to 4
- crossing: int32 [8, 512], P('tile'), may hold values from 0 to 63
- bins: int32 [4], P('freq'), may hold values from 8 to 71
- transmission: float32 [4, 2, 64], P('freq'), may hold values from -1 to 1
- capture: bfloat16 [4, 2, 512, 512], P('freq', None, 'tile'), may hold values from -0.01171875 to 0.01171875
Outputs:
- image: float32 [2, 8, 512], P(None, 'tile')
The draws below stay inside these ranges and needn't reach their ends.
All inputs are finite; a program needn't handle non-finite values.
Results may differ from the reference program's by a relative error of at most 0.0033.
Values may be sent and summed in bfloat16 or wider, within the bound.
No kernel may reach another device: no remote copies, remote signals or barrier semaphores. Data moves between devices by JAX's collectives and lax.ppermute only.
A program may use at most 64 MiB of HBM per device.

```python
import math
import jax
import jax.numpy as jnp
from jax import lax

ELEMENTS = 512
CROSSINGS = 64
FREQS = 4
SLAB_ROWS = 8
SLAB_COLS = 512


def with_ends(values, rng, smallest, largest):
    extent = values.shape
    spot = [jax.random.randint(jax.random.fold_in(rng, axis), (), 0, extent[axis]) for axis in range(len(extent))]
    values = values.at[tuple(spot)].set(smallest)
    longest = extent.index(max(extent))
    spot[longest] = (spot[longest] + 1) % extent[longest]
    return values.at[tuple(spot)].set(largest)


def levels(key, extent, shards, smallest, top_value):
    def one(dim, parts):
        heights = jax.random.uniform(jax.random.fold_in(jax.random.fold_in(key, 6), dim), (parts,), jnp.float32, smallest / len(shards), top_value / len(shards))
        return jnp.repeat(jnp.exp(heights), extent[dim] // parts).reshape((-1,) + (1,) * (len(extent) - dim - 1))

    gain = one(*shards[0])
    for cut in shards[1:]:
        gain = gain * one(*cut)
    return gain


def centred(stream_key, extent, spread, most, shards=(), kind=jnp.bfloat16):
    level = levels(stream_key, extent, shards, -0.22, 0.18) if shards else 1.0
    result = jax.random.normal(stream_key, extent, jnp.float32) * spread * level
    return jnp.minimum(jnp.maximum(result, -most), most).astype(kind)


def setup_inputs(seed: int = 0) -> dict:
    streams_of = jax.random.split(jax.random.key(seed), 6)
    travel_time = jnp.clip(4.0 * jax.random.uniform(streams_of[0], (ELEMENTS, SLAB_ROWS, SLAB_COLS), jnp.float32) ** levels(streams_of[0], (ELEMENTS, SLAB_ROWS, SLAB_COLS), ((0, 8), (2, 4)), -0.2, 0.2), 0.0, 4.0)
    crossing = with_ends(jax.random.randint(streams_of[1], (SLAB_ROWS, SLAB_COLS), 0, CROSSINGS), jax.random.fold_in(streams_of[1], 1), 0, CROSSINGS - 1).astype(jnp.int32)
    bins = with_ends(jax.random.randint(streams_of[2], (FREQS,), 8, 72), jax.random.fold_in(streams_of[2], 1), 8, 71).astype(jnp.int32)
    transmission = jnp.clip(jax.random.uniform(streams_of[3], (FREQS, 2, CROSSINGS), jnp.float32, -1.0, 1.0) * levels(streams_of[3], (FREQS, 2, CROSSINGS), ((0, 4),), -0.4, 0.0), -1.0, 1.0)
    capture = centred(streams_of[4], (FREQS, 2, ELEMENTS, ELEMENTS), (ELEMENTS * ELEMENTS) ** -0.5, 0.01171875, ((0, 4), (2, 8)))
    return dict(travel_time=travel_time, crossing=crossing, bins=bins, transmission=transmission, capture=capture)


TWO_PI = 2.0 * math.pi


def one_frequency(travel_time, crossing, bin_value, trans, capture_f):
    angle = (TWO_PI * bin_value.astype(jnp.float32)) * travel_time
    field_real = jnp.cos(angle).astype(jnp.bfloat16)
    field_imag = (-jnp.sin(angle)).astype(jnp.bfloat16)
    elements = travel_time.shape[0]
    field_real = field_real.reshape(elements, -1)
    field_imag = field_imag.reshape(elements, -1)
    cap_real = capture_f[0]
    cap_imag = capture_f[1]
    w_real = jnp.dot(cap_real, field_real, preferred_element_type=jnp.float32) - jnp.dot(cap_imag, field_imag, preferred_element_type=jnp.float32)
    w_imag = jnp.dot(cap_real, field_imag, preferred_element_type=jnp.float32) + jnp.dot(cap_imag, field_real, preferred_element_type=jnp.float32)
    g_real = field_real.astype(jnp.float32)
    g_imag = field_imag.astype(jnp.float32)
    focus_real = jnp.sum(g_real * w_real - g_imag * w_imag, axis=0)
    focus_imag = jnp.sum(g_real * w_imag + g_imag * w_real, axis=0)
    flat_cross = crossing.reshape(-1)
    cells = trans.shape[1]
    match = flat_cross[None, :] == jnp.arange(cells, dtype=jnp.int32)[:, None]
    coeff_real = jnp.sum(jnp.where(match, trans[0][:, None], jnp.float32(0.0)), axis=0)
    coeff_imag = jnp.sum(jnp.where(match, trans[1][:, None], jnp.float32(0.0)), axis=0)
    square_real = coeff_real * coeff_real - coeff_imag * coeff_imag
    square_imag = 2.0 * coeff_real * coeff_imag
    part_real = square_real * focus_real - square_imag * focus_imag
    part_imag = square_real * focus_imag + square_imag * focus_real
    return jnp.stack([part_real, part_imag]).reshape((2,) + crossing.shape)


def reference(travel_time, crossing, bins, transmission, capture):
    def step(total, inputs):
        bin_value, trans, capture_f = inputs
        return total + one_frequency(travel_time, crossing, bin_value, trans, capture_f), None

    start = jnp.zeros((2,) + crossing.shape, jnp.float32)
    image, unused = lax.scan(step, start, (bins, transmission, capture))
    return image
```

```python
import math

import jax
import jax.numpy as jnp
from jax import lax
from jax.sharding import PartitionSpec as P

TWO_PI = 2.0 * math.pi


def gather_shifted(block, axis_name, size):
    pieces = [block]
    for s in range(1, size):
        pairs = [(i, (i - s) % size) for i in range(size)]
        pieces.append(lax.ppermute(block, axis_name, pairs))
    return pieces


def all_sum(value, axis_name, size):
    step = 1
    while step < size:
        pairs = [(i, i ^ step) for i in range(size)]
        value = value + lax.ppermute(value, axis_name, pairs)
        step *= 2
    return value


def body(travel_time, crossing, bins, transmission, capture):
    tiles = lax.axis_size("tile")
    freqs = lax.axis_size("freq")
    k = lax.axis_index("tile")
    f = lax.axis_index("freq")

    cap_pieces = gather_shifted(capture[0], "tile", tiles)
    cap_perm = jnp.concatenate(cap_pieces, axis=1)
    rows = cap_perm.shape[1]
    own = capture.shape[2]
    cap_real = cap_perm[0]
    cap_imag = cap_perm[1]

    regrouped = lax.all_to_all(travel_time, "tile", split_axis=1, concat_axis=0, tiled=True)
    col_pieces = gather_shifted(regrouped, "freq", freqs)
    view = jnp.stack(col_pieces, axis=2)
    elements, row_count, _, width = view.shape
    voxels = row_count * freqs * width

    scaled = TWO_PI * bins[0].astype(jnp.float32)
    angle = scaled * view.reshape(elements, voxels)
    field_real = jnp.cos(angle).astype(jnp.bfloat16)
    field_imag = (-jnp.sin(angle)).astype(jnp.bfloat16)
    stacked = jnp.concatenate([field_real, field_imag], axis=0)

    block = jnp.concatenate(
        [
            jnp.concatenate([cap_real, -cap_imag], axis=1),
            jnp.concatenate([cap_imag, cap_real], axis=1),
        ],
        axis=0,
    )
    product = jnp.dot(block, stacked, preferred_element_type=jnp.float32)
    w_real = product[:rows]
    w_imag = product[rows:]

    start = k * own
    g_real = lax.dynamic_slice_in_dim(jnp.concatenate([field_real, field_real], axis=0), start, rows, 0)
    g_imag = lax.dynamic_slice_in_dim(jnp.concatenate([field_imag, field_imag], axis=0), start, rows, 0)
    g_real = g_real.astype(jnp.float32)
    g_imag = g_imag.astype(jnp.float32)
    focus_real = jnp.sum(g_real * w_real - g_imag * w_imag, axis=0)
    focus_imag = jnp.sum(g_real * w_imag + g_imag * w_real, axis=0)

    focus = jnp.stack([focus_real, focus_imag]).reshape(2, row_count, freqs, width)
    focus = jnp.roll(focus, f, axis=2).reshape(2, row_count, freqs * width)
    focus_real = focus[0]
    focus_imag = focus[1]

    cells = transmission.shape[2]
    match = crossing[None] == lax.broadcasted_iota(jnp.int32, (cells, 1, 1), 0)
    coeff_real = jnp.sum(jnp.where(match, transmission[0, 0][:, None, None], jnp.float32(0.0)), axis=0)
    coeff_imag = jnp.sum(jnp.where(match, transmission[0, 1][:, None, None], jnp.float32(0.0)), axis=0)
    square_real = coeff_real * coeff_real - coeff_imag * coeff_imag
    square_imag = 2.0 * coeff_real * coeff_imag
    part_real = square_real * focus_real - square_imag * focus_imag
    part_imag = square_real * focus_imag + square_imag * focus_real
    partial_image = jnp.stack([part_real, part_imag])
    return all_sum(partial_image, "freq", freqs)


def solution(mesh):
    in_specs = (
        P("tile", None, "freq"),
        P("tile", None),
        P("freq"),
        P("freq", None, None),
        P("freq", None, "tile", None),
    )
    out_specs = P(None, "tile", None)
    return jax.shard_map(body, mesh=mesh, in_specs=in_specs, out_specs=out_specs, check_vma=False)
```

```python
import math

import jax
import jax.numpy as jnp
from jax import lax
from jax.sharding import PartitionSpec as P

TWO_PI = 2.0 * math.pi


def gather_shifted(block, axis_name, size):
    pieces = [block]
    for s in range(1, size):
        pairs = [(i, (i - s) % size) for i in range(size)]
        pieces.append(lax.ppermute(block, axis_name, pairs))
    return pieces


def chain(block, axis_name, size, stride, step, direction):
    positions = size // stride
    pairs = []
    for z in range(positions):
        target = z + direction
        if 0 <= target < positions and 0 <= z - direction * (step - 1) < positions:
            pairs += [(z * stride + y, target * stride + y) for y in range(stride)]
    return lax.ppermute(block, axis_name, pairs)


def line_gather(block, axis_name, size):
    positions = size // 2
    z = lax.axis_index(axis_name) // 2
    left = [block]
    right = [block]
    for j in range(1, positions):
        left.append(chain(left[-1], axis_name, size, 2, j, 1))
        right.append(chain(right[-1], axis_name, size, 2, j, -1))
    slots = left[:0:-1] + [block] + right[1:]
    return slots, z


def pair_swap(slots, axis_name, size):
    positions = size // 2
    centre = positions - 1
    out = []
    for i, piece in enumerate(slots):
        d = i - centre
        pairs = [(p * 2 + y, p * 2 + 1 - y) for p in range(positions) if 0 <= p + d < positions for y in range(2)]
        out.append(lax.ppermute(piece, axis_name, pairs))
    return out


def gather_rows(block, axis_name, size):
    positions = size // 2
    slots, z = line_gather(block, axis_name, size)
    other = pair_swap(slots, axis_name, size)
    mine = lax.dynamic_slice_in_dim(jnp.stack(slots), positions - 1 - z, positions, 0)
    theirs = lax.dynamic_slice_in_dim(jnp.stack(other), positions - 1 - z, positions, 0)
    both = jnp.stack([mine, theirs], axis=1)
    both = jnp.roll(both, lax.axis_index(axis_name) % 2, axis=1)
    return both.reshape((size,) + block.shape)


def gather_columns(block, axis_name, size):
    outer = size // 2
    same_core = [block]
    for s in range(1, outer):
        pairs = [(i, (i - 2 * s) % size) for i in range(size)]
        same_core.append(lax.ppermute(block, axis_name, pairs))
    swap = [(i, i ^ 1) for i in range(size)]
    partner = [lax.ppermute(piece, axis_name, swap) for piece in same_core]
    return jnp.stack([jnp.stack(same_core), jnp.stack(partner)], axis=1)


def all_sum(value, axis_name, size):
    step = 1
    while step < size:
        pairs = [(i, i ^ step) for i in range(size)]
        value = value + lax.ppermute(value, axis_name, pairs)
        step *= 2
    return value


def body(travel_time, crossing, bins, transmission, capture):
    tiles = lax.axis_size("tile")
    freqs = lax.axis_size("freq")
    k = lax.axis_index("tile")
    f = lax.axis_index("freq")

    cap_all = gather_rows(capture[0], "tile", tiles)
    cap_all = jnp.moveaxis(cap_all, 0, 1)
    cap_real = cap_all[0].reshape(-1, cap_all.shape[-1])
    cap_imag = cap_all[1].reshape(-1, cap_all.shape[-1])
    rows = cap_real.shape[0]

    regrouped = lax.all_to_all(travel_time, "tile", split_axis=1, concat_axis=0, tiled=True)
    view = gather_columns(regrouped, "freq", freqs)
    view = jnp.moveaxis(view.reshape((freqs,) + regrouped.shape), 0, 2)
    elements, row_count, _, width = view.shape
    voxels = row_count * freqs * width

    scaled = TWO_PI * bins[0].astype(jnp.float32)
    angle = scaled * view.reshape(elements, voxels)
    field_real = jnp.cos(angle).astype(jnp.bfloat16)
    field_imag = (-jnp.sin(angle)).astype(jnp.bfloat16)
    stacked = jnp.concatenate([field_real, field_imag], axis=0)

    block = jnp.concatenate(
        [
            jnp.concatenate([cap_real, -cap_imag], axis=1),
            jnp.concatenate([cap_imag, cap_real], axis=1),
        ],
        axis=0,
    )
    product = jnp.dot(block, stacked, preferred_element_type=jnp.float32)
    w_real = product[:rows]
    w_imag = product[rows:]

    g_real = field_real.astype(jnp.float32)
    g_imag = field_imag.astype(jnp.float32)
    focus_real = jnp.sum(g_real * w_real - g_imag * w_imag, axis=0)
    focus_imag = jnp.sum(g_real * w_imag + g_imag * w_real, axis=0)

    outer = freqs // 2
    focus = jnp.stack([focus_real, focus_imag]).reshape(2, row_count, outer, 2, width)
    focus = jnp.roll(focus, f % 2, axis=3)
    focus = jnp.roll(focus, f // 2, axis=2).reshape(2, row_count, freqs * width)
    focus_real = focus[0]
    focus_imag = focus[1]

    cells = transmission.shape[2]
    match = crossing[None] == lax.broadcasted_iota(jnp.int32, (cells, 1, 1), 0)
    coeff_real = jnp.sum(jnp.where(match, transmission[0, 0][:, None, None], jnp.float32(0.0)), axis=0)
    coeff_imag = jnp.sum(jnp.where(match, transmission[0, 1][:, None, None], jnp.float32(0.0)), axis=0)
    square_real = coeff_real * coeff_real - coeff_imag * coeff_imag
    square_imag = 2.0 * coeff_real * coeff_imag
    part_real = square_real * focus_real - square_imag * focus_imag
    part_imag = square_real * focus_imag + square_imag * focus_real
    partial_image = jnp.stack([part_real, part_imag])
    return all_sum(partial_image, "freq", freqs)


def solution(mesh):
    in_specs = (
        P("tile", None, "freq"),
        P("tile", None),
        P("freq"),
        P("freq", None, None),
        P("freq", None, "tile", None),
    )
    out_specs = P(None, "tile", None)
    return jax.shard_map(body, mesh=mesh, in_specs=in_specs, out_specs=out_specs, check_vma=False)
```

```python
import math

import jax
import jax.numpy as jnp
from jax import lax
from jax.sharding import PartitionSpec as P

TWO_PI = 2.0 * math.pi


def gather_shifted(block, axis_name, size):
    pieces = [block]
    for s in range(1, size):
        pairs = [(i, (i - s) % size) for i in range(size)]
        pieces.append(lax.ppermute(block, axis_name, pairs))
    return pieces


def chain(block, axis_name, size, stride, step, direction):
    positions = size // stride
    pairs = []
    for z in range(positions):
        target = z + direction
        if 0 <= target < positions and 0 <= z - direction * (step - 1) < positions:
            pairs += [(z * stride + y, target * stride + y) for y in range(stride)]
    return lax.ppermute(block, axis_name, pairs)


def line_gather(block, axis_name, size):
    positions = size // 2
    z = lax.axis_index(axis_name) // 2
    left = [block]
    right = [block]
    for j in range(1, positions):
        left.append(chain(left[-1], axis_name, size, 2, j, 1))
        right.append(chain(right[-1], axis_name, size, 2, j, -1))
    slots = left[:0:-1] + [block] + right[1:]
    return slots, z


def pair_swap(slots, axis_name, size):
    positions = size // 2
    centre = positions - 1
    out = []
    for i, piece in enumerate(slots):
        d = i - centre
        pairs = [(p * 2 + y, p * 2 + 1 - y) for p in range(positions) if 0 <= p + d < positions for y in range(2)]
        out.append(lax.ppermute(piece, axis_name, pairs))
    return out


def gather_rows(block, axis_name, size):
    positions = size // 2
    slots, z = line_gather(block, axis_name, size)
    other = pair_swap(slots, axis_name, size)
    mine = lax.dynamic_slice_in_dim(jnp.stack(slots), positions - 1 - z, positions, 0)
    theirs = lax.dynamic_slice_in_dim(jnp.stack(other), positions - 1 - z, positions, 0)
    both = jnp.stack([mine, theirs], axis=1)
    both = jnp.roll(both, lax.axis_index(axis_name) % 2, axis=1)
    return both.reshape((size,) + block.shape)


def gather_columns(block, axis_name, size):
    outer = size // 2
    same_core = [block]
    for s in range(1, outer):
        pairs = [(i, (i - 2 * s) % size) for i in range(size)]
        same_core.append(lax.ppermute(block, axis_name, pairs))
    swap = [(i, i ^ 1) for i in range(size)]
    partner = [lax.ppermute(piece, axis_name, swap) for piece in same_core]
    return jnp.stack([jnp.stack(same_core), jnp.stack(partner)], axis=1)


def all_sum(value, axis_name, size):
    step = 1
    while step < size:
        pairs = [(i, i ^ step) for i in range(size)]
        value = value + lax.ppermute(value, axis_name, pairs)
        step *= 2
    return value


def body(travel_time, crossing, bins, transmission, capture):
    tiles = lax.axis_size("tile")
    freqs = lax.axis_size("freq")
    k = lax.axis_index("tile")
    f = lax.axis_index("freq")

    regrouped = lax.all_to_all(travel_time, "tile", split_axis=1, concat_axis=0, tiled=True)
    view = gather_columns(regrouped, "freq", freqs)
    view = jnp.moveaxis(view.reshape((freqs,) + regrouped.shape), 0, 2)
    elements, row_count, _, width = view.shape
    voxels = row_count * freqs * width

    scaled = TWO_PI * bins[0].astype(jnp.float32)
    angle = scaled * view.reshape(elements, voxels)
    field_real = jnp.cos(angle).astype(jnp.bfloat16)
    field_imag = (-jnp.sin(angle)).astype(jnp.bfloat16)
    left = jnp.concatenate([field_real, field_imag], axis=1)
    right = jnp.concatenate([-field_imag, field_real], axis=1)

    cap_pieces = gather_shifted(capture[0], "tile", tiles)
    own = capture.shape[2]
    focus_real = None
    for s, piece in enumerate(cap_pieces):
        product = jnp.dot(piece[0], left, preferred_element_type=jnp.float32) + jnp.dot(
            piece[1], right, preferred_element_type=jnp.float32
        )
        w_real = product[:, :voxels]
        w_imag = product[:, voxels:]
        start = ((k + s) % tiles) * own
        g_real = lax.dynamic_slice_in_dim(field_real, start, own, 0).astype(jnp.float32)
        g_imag = lax.dynamic_slice_in_dim(field_imag, start, own, 0).astype(jnp.float32)
        part_real = jnp.sum(g_real * w_real - g_imag * w_imag, axis=0)
        part_imag = jnp.sum(g_real * w_imag + g_imag * w_real, axis=0)
        if focus_real is None:
            focus_real, focus_imag = part_real, part_imag
        else:
            focus_real = focus_real + part_real
            focus_imag = focus_imag + part_imag

    outer = freqs // 2
    focus = jnp.stack([focus_real, focus_imag]).reshape(2, row_count, outer, 2, width)
    focus = jnp.roll(focus, f % 2, axis=3)
    focus = jnp.roll(focus, f // 2, axis=2).reshape(2, row_count, freqs * width)
    focus_real = focus[0]
    focus_imag = focus[1]

    cells = transmission.shape[2]
    match = crossing[None] == lax.broadcasted_iota(jnp.int32, (cells, 1, 1), 0)
    coeff_real = jnp.sum(jnp.where(match, transmission[0, 0][:, None, None], jnp.float32(0.0)), axis=0)
    coeff_imag = jnp.sum(jnp.where(match, transmission[0, 1][:, None, None], jnp.float32(0.0)), axis=0)
    square_real = coeff_real * coeff_real - coeff_imag * coeff_imag
    square_imag = 2.0 * coeff_real * coeff_imag
    part_real = square_real * focus_real - square_imag * focus_imag
    part_imag = square_real * focus_imag + square_imag * focus_real
    partial_image = jnp.stack([part_real, part_imag])
    return all_sum(partial_image, "freq", freqs)


def solution(mesh):
    in_specs = (
        P("tile", None, "freq"),
        P("tile", None),
        P("freq"),
        P("freq", None, None),
        P("freq", None, "tile", None),
    )
    out_specs = P(None, "tile", None)
    return jax.shard_map(body, mesh=mesh, in_specs=in_specs, out_specs=out_specs, check_vma=False)
```

```python
import math

import jax
import jax.numpy as jnp
from jax import lax
from jax.sharding import PartitionSpec as P

TWO_PI = 2.0 * math.pi


def gather_shifted(block, axis_name, size):
    pieces = [block]
    for s in range(1, size):
        pairs = [(i, (i - s) % size) for i in range(size)]
        pieces.append(lax.ppermute(block, axis_name, pairs))
    return pieces


def chain(block, axis_name, size, stride, step, direction):
    positions = size // stride
    pairs = []
    for z in range(positions):
        target = z + direction
        if 0 <= target < positions and 0 <= z - direction * (step - 1) < positions:
            pairs += [(z * stride + y, target * stride + y) for y in range(stride)]
    return lax.ppermute(block, axis_name, pairs)


def line_gather(block, axis_name, size):
    positions = size // 2
    z = lax.axis_index(axis_name) // 2
    left = [block]
    right = [block]
    for j in range(1, positions):
        left.append(chain(left[-1], axis_name, size, 2, j, 1))
        right.append(chain(right[-1], axis_name, size, 2, j, -1))
    slots = left[:0:-1] + [block] + right[1:]
    return slots, z


def pair_swap(slots, axis_name, size):
    positions = size // 2
    centre = positions - 1
    out = []
    for i, piece in enumerate(slots):
        d = i - centre
        pairs = [(p * 2 + y, p * 2 + 1 - y) for p in range(positions) if 0 <= p + d < positions for y in range(2)]
        out.append(lax.ppermute(piece, axis_name, pairs))
    return out


def gather_rows(block, axis_name, size):
    positions = size // 2
    slots, z = line_gather(block, axis_name, size)
    other = pair_swap(slots, axis_name, size)
    mine = lax.dynamic_slice_in_dim(jnp.stack(slots), positions - 1 - z, positions, 0)
    theirs = lax.dynamic_slice_in_dim(jnp.stack(other), positions - 1 - z, positions, 0)
    both = jnp.stack([mine, theirs], axis=1)
    both = jnp.roll(both, lax.axis_index(axis_name) % 2, axis=1)
    return both.reshape((size,) + block.shape)


def gather_columns(block, axis_name, size):
    outer = size // 2
    same_core = [block]
    for s in range(1, outer):
        pairs = [(i, (i - 2 * s) % size) for i in range(size)]
        same_core.append(lax.ppermute(block, axis_name, pairs))
    swap = [(i, i ^ 1) for i in range(size)]
    partner = [lax.ppermute(piece, axis_name, swap) for piece in same_core]
    return jnp.stack([jnp.stack(same_core), jnp.stack(partner)], axis=1)


def gather_row_blocks(block, axis_name, size):
    positions = size // 2
    i = lax.axis_index(axis_name)
    z = i // 2
    y = i % 2
    row = [block]
    for s in range(1, positions):
        pairs = [(p * 2 + r, ((p - s) % positions) * 2 + r) for p in range(positions) for r in range(2)]
        row.append(lax.ppermute(block, axis_name, pairs))
    other = lax.ppermute(jnp.stack(row), axis_name, [(j, j ^ 1) for j in range(size)])
    out = []
    for s in range(positions):
        out.append((((z + s) % positions) * 2 + y, row[s]))
        out.append((((z + s) % positions) * 2 + 1 - y, other[s]))
    return out


def all_sum_once(value, axis_name, size):
    pieces = gather_shifted(value, axis_name, size)
    stacked = jnp.roll(jnp.stack(pieces), lax.axis_index(axis_name), axis=0)
    total = stacked[0]
    for j in range(1, size):
        total = total + stacked[j]
    return total


def all_sum(value, axis_name, size):
    step = 1
    while step < size:
        pairs = [(i, i ^ step) for i in range(size)]
        value = value + lax.ppermute(value, axis_name, pairs)
        step *= 2
    return value


def body(travel_time, crossing, bins, transmission, capture):
    tiles = lax.axis_size("tile")
    freqs = lax.axis_size("freq")
    k = lax.axis_index("tile")
    f = lax.axis_index("freq")

    regrouped = lax.all_to_all(travel_time, "tile", split_axis=1, concat_axis=0, tiled=True)
    view = gather_columns(regrouped, "freq", freqs)
    view = jnp.moveaxis(view.reshape((freqs,) + regrouped.shape), 0, 2)
    elements, row_count, _, width = view.shape
    voxels = row_count * freqs * width

    scaled = TWO_PI * bins[0].astype(jnp.float32)
    angle = scaled * view.reshape(elements, voxels)
    field_real = jnp.cos(angle).astype(jnp.bfloat16)
    field_imag = (-jnp.sin(angle)).astype(jnp.bfloat16)
    left = jnp.concatenate([field_real, field_imag], axis=1)
    right = jnp.concatenate([-field_imag, field_real], axis=1)

    cap_pieces = gather_row_blocks(capture[0], "tile", tiles)
    own = capture.shape[2]
    focus_real = None
    for index, piece in cap_pieces:
        product = jnp.dot(piece[0], left, preferred_element_type=jnp.float32) + jnp.dot(
            piece[1], right, preferred_element_type=jnp.float32
        )
        w_real = product[:, :voxels]
        w_imag = product[:, voxels:]
        start = index * own
        g_real = lax.dynamic_slice_in_dim(field_real, start, own, 0).astype(jnp.float32)
        g_imag = lax.dynamic_slice_in_dim(field_imag, start, own, 0).astype(jnp.float32)
        part_real = jnp.sum(g_real * w_real - g_imag * w_imag, axis=0)
        part_imag = jnp.sum(g_real * w_imag + g_imag * w_real, axis=0)
        if focus_real is None:
            focus_real, focus_imag = part_real, part_imag
        else:
            focus_real = focus_real + part_real
            focus_imag = focus_imag + part_imag

    outer = freqs // 2
    focus = jnp.stack([focus_real, focus_imag]).reshape(2, row_count, outer, 2, width)
    focus = jnp.roll(focus, f % 2, axis=3)
    focus = jnp.roll(focus, f // 2, axis=2).reshape(2, row_count, freqs * width)
    focus_real = focus[0]
    focus_imag = focus[1]

    cells = transmission.shape[2]
    match = crossing[None] == lax.broadcasted_iota(jnp.int32, (cells, 1, 1), 0)
    coeff_real = jnp.sum(jnp.where(match, transmission[0, 0][:, None, None], jnp.float32(0.0)), axis=0)
    coeff_imag = jnp.sum(jnp.where(match, transmission[0, 1][:, None, None], jnp.float32(0.0)), axis=0)
    square_real = coeff_real * coeff_real - coeff_imag * coeff_imag
    square_imag = 2.0 * coeff_real * coeff_imag
    part_real = square_real * focus_real - square_imag * focus_imag
    part_imag = square_real * focus_imag + square_imag * focus_real
    partial_image = jnp.stack([part_real, part_imag])
    return all_sum_once(partial_image, "freq", freqs)


def solution(mesh):
    in_specs = (
        P("tile", None, "freq"),
        P("tile", None),
        P("freq"),
        P("freq", None, None),
        P("freq", None, "tile", None),
    )
    out_specs = P(None, "tile", None)
    return jax.shard_map(body, mesh=mesh, in_specs=in_specs, out_specs=out_specs, check_vma=False)
```

```python
import math

import jax
import jax.numpy as jnp
from jax import lax
from jax.sharding import PartitionSpec as P

TWO_PI = 2.0 * math.pi


def gather_shifted(block, axis_name, size):
    pieces = [block]
    for s in range(1, size):
        pairs = [(i, (i - s) % size) for i in range(size)]
        pieces.append(lax.ppermute(block, axis_name, pairs))
    return pieces


def chain(block, axis_name, size, stride, step, direction):
    positions = size // stride
    pairs = []
    for z in range(positions):
        target = z + direction
        if 0 <= target < positions and 0 <= z - direction * (step - 1) < positions:
            pairs += [(z * stride + y, target * stride + y) for y in range(stride)]
    return lax.ppermute(block, axis_name, pairs)


def line_gather(block, axis_name, size):
    positions = size // 2
    z = lax.axis_index(axis_name) // 2
    left = [block]
    right = [block]
    for j in range(1, positions):
        left.append(chain(left[-1], axis_name, size, 2, j, 1))
        right.append(chain(right[-1], axis_name, size, 2, j, -1))
    slots = left[:0:-1] + [block] + right[1:]
    return slots, z


def pair_swap(slots, axis_name, size):
    positions = size // 2
    centre = positions - 1
    out = []
    for i, piece in enumerate(slots):
        d = i - centre
        pairs = [(p * 2 + y, p * 2 + 1 - y) for p in range(positions) if 0 <= p + d < positions for y in range(2)]
        out.append(lax.ppermute(piece, axis_name, pairs))
    return out


def gather_rows(block, axis_name, size):
    positions = size // 2
    slots, z = line_gather(block, axis_name, size)
    other = pair_swap(slots, axis_name, size)
    mine = lax.dynamic_slice_in_dim(jnp.stack(slots), positions - 1 - z, positions, 0)
    theirs = lax.dynamic_slice_in_dim(jnp.stack(other), positions - 1 - z, positions, 0)
    both = jnp.stack([mine, theirs], axis=1)
    both = jnp.roll(both, lax.axis_index(axis_name) % 2, axis=1)
    return both.reshape((size,) + block.shape)


def gather_columns(block, axis_name, size):
    outer = size // 2
    same_core = [block]
    for s in range(1, outer):
        pairs = [(i, (i - 2 * s) % size) for i in range(size)]
        same_core.append(lax.ppermute(block, axis_name, pairs))
    swap = [(i, i ^ 1) for i in range(size)]
    partner = [lax.ppermute(piece, axis_name, swap) for piece in same_core]
    return jnp.stack([jnp.stack(same_core), jnp.stack(partner)], axis=1)


def gather_row_blocks(block, axis_name, size):
    positions = size // 2
    i = lax.axis_index(axis_name)
    z = i // 2
    y = i % 2
    row = [block]
    for s in range(1, positions):
        pairs = [(p * 2 + r, ((p - s) % positions) * 2 + r) for p in range(positions) for r in range(2)]
        row.append(lax.ppermute(block, axis_name, pairs))
    other = lax.ppermute(jnp.stack(row), axis_name, [(j, j ^ 1) for j in range(size)])
    out = []
    for s in range(positions):
        out.append((((z + s) % positions) * 2 + y, row[s]))
        out.append((((z + s) % positions) * 2 + 1 - y, other[s]))
    return out


def all_sum_once(value, axis_name, size):
    pieces = gather_shifted(value, axis_name, size)
    stacked = jnp.roll(jnp.stack(pieces), lax.axis_index(axis_name), axis=0)
    total = stacked[0]
    for j in range(1, size):
        total = total + stacked[j]
    return total


def all_sum(value, axis_name, size):
    step = 1
    while step < size:
        pairs = [(i, i ^ step) for i in range(size)]
        value = value + lax.ppermute(value, axis_name, pairs)
        step *= 2
    return value


def body(travel_time, crossing, bins, transmission, capture):
    tiles = lax.axis_size("tile")
    freqs = lax.axis_size("freq")
    k = lax.axis_index("tile")
    f = lax.axis_index("freq")

    regrouped = lax.all_to_all(travel_time, "tile", split_axis=1, concat_axis=0, tiled=True)
    view = gather_columns(regrouped, "freq", freqs)
    view = jnp.moveaxis(view.reshape((freqs,) + regrouped.shape), 0, 2)
    elements, row_count, _, width = view.shape
    voxels = row_count * freqs * width

    scaled = TWO_PI * bins[0].astype(jnp.float32)
    angle = scaled * view.reshape(elements, voxels)
    field_real = jnp.cos(angle).astype(jnp.bfloat16)
    field_imag = (-jnp.sin(angle)).astype(jnp.bfloat16)
    left = jnp.concatenate([field_real, field_imag], axis=1)
    right = jnp.concatenate([-field_imag, field_real], axis=1)

    positions = tiles // 2
    z = k // 2
    y = k % 2
    row = [capture[0]]
    for s in range(1, positions):
        pairs = [(p * 2 + r, ((p - s) % positions) * 2 + r) for p in range(positions) for r in range(2)]
        row.append(lax.ppermute(capture[0], "tile", pairs))
    row = jnp.stack(row)
    other = lax.ppermute(row, "tile", [(j, j ^ 1) for j in range(tiles)])

    def partial_focus(group, which_row):
        own = group.shape[2]
        cap_real = group[:, 0].reshape(-1, group.shape[-1])
        cap_imag = group[:, 1].reshape(-1, group.shape[-1])
        product = jnp.dot(cap_real, left, preferred_element_type=jnp.float32) + jnp.dot(
            cap_imag, right, preferred_element_type=jnp.float32
        )
        w_real = product[:, :voxels]
        w_imag = product[:, voxels:]

        def rows_of(field):
            grid = field.reshape(positions, 2, own, voxels)
            picked = lax.dynamic_index_in_dim(grid, which_row, 1, keepdims=False)
            picked = jnp.roll(picked, -z, axis=0)
            return picked.reshape(-1, voxels).astype(jnp.float32)

        g_real = rows_of(field_real)
        g_imag = rows_of(field_imag)
        part_real = jnp.sum(g_real * w_real - g_imag * w_imag, axis=0)
        part_imag = jnp.sum(g_real * w_imag + g_imag * w_real, axis=0)
        return part_real, part_imag

    mine_real, mine_imag = partial_focus(row, y)
    mine_real, mine_imag, other = lax.optimization_barrier((mine_real, mine_imag, other))
    theirs_real, theirs_imag = partial_focus(other, 1 - y)
    focus_real = mine_real + theirs_real
    focus_imag = mine_imag + theirs_imag

    outer = freqs // 2
    focus = jnp.stack([focus_real, focus_imag]).reshape(2, row_count, outer, 2, width)
    focus = jnp.roll(focus, f % 2, axis=3)
    focus = jnp.roll(focus, f // 2, axis=2).reshape(2, row_count, freqs * width)
    focus_real = focus[0]
    focus_imag = focus[1]

    cells = transmission.shape[2]
    match = crossing[None] == lax.broadcasted_iota(jnp.int32, (cells, 1, 1), 0)
    coeff_real = jnp.sum(jnp.where(match, transmission[0, 0][:, None, None], jnp.float32(0.0)), axis=0)
    coeff_imag = jnp.sum(jnp.where(match, transmission[0, 1][:, None, None], jnp.float32(0.0)), axis=0)
    square_real = coeff_real * coeff_real - coeff_imag * coeff_imag
    square_imag = 2.0 * coeff_real * coeff_imag
    part_real = square_real * focus_real - square_imag * focus_imag
    part_imag = square_real * focus_imag + square_imag * focus_real
    partial_image = jnp.stack([part_real, part_imag])
    return all_sum_once(partial_image, "freq", freqs)


def solution(mesh):
    in_specs = (
        P("tile", None, "freq"),
        P("tile", None),
        P("freq"),
        P("freq", None, None),
        P("freq", None, "tile", None),
    )
    out_specs = P(None, "tile", None)
    return jax.shard_map(body, mesh=mesh, in_specs=in_specs, out_specs=out_specs, check_vma=False)
```

```python
import math

import jax
import jax.numpy as jnp
from jax import lax
from jax.sharding import PartitionSpec as P

TWO_PI = 2.0 * math.pi


def gather_shifted(block, axis_name, size):
    pieces = [block]
    for s in range(1, size):
        pairs = [(i, (i - s) % size) for i in range(size)]
        pieces.append(lax.ppermute(block, axis_name, pairs))
    return pieces


def chain(block, axis_name, size, stride, step, direction):
    positions = size // stride
    pairs = []
    for z in range(positions):
        target = z + direction
        if 0 <= target < positions and 0 <= z - direction * (step - 1) < positions:
            pairs += [(z * stride + y, target * stride + y) for y in range(stride)]
    return lax.ppermute(block, axis_name, pairs)


def line_gather(block, axis_name, size):
    positions = size // 2
    z = lax.axis_index(axis_name) // 2
    left = [block]
    right = [block]
    for j in range(1, positions):
        left.append(chain(left[-1], axis_name, size, 2, j, 1))
        right.append(chain(right[-1], axis_name, size, 2, j, -1))
    slots = left[:0:-1] + [block] + right[1:]
    return slots, z


def pair_swap(slots, axis_name, size):
    positions = size // 2
    centre = positions - 1
    out = []
    for i, piece in enumerate(slots):
        d = i - centre
        pairs = [(p * 2 + y, p * 2 + 1 - y) for p in range(positions) if 0 <= p + d < positions for y in range(2)]
        out.append(lax.ppermute(piece, axis_name, pairs))
    return out


def gather_rows(block, axis_name, size):
    positions = size // 2
    slots, z = line_gather(block, axis_name, size)
    other = pair_swap(slots, axis_name, size)
    mine = lax.dynamic_slice_in_dim(jnp.stack(slots), positions - 1 - z, positions, 0)
    theirs = lax.dynamic_slice_in_dim(jnp.stack(other), positions - 1 - z, positions, 0)
    both = jnp.stack([mine, theirs], axis=1)
    both = jnp.roll(both, lax.axis_index(axis_name) % 2, axis=1)
    return both.reshape((size,) + block.shape)


def gather_columns(block, axis_name, size):
    outer = size // 2
    same_core = [block]
    for s in range(1, outer):
        pairs = [(i, (i - 2 * s) % size) for i in range(size)]
        same_core.append(lax.ppermute(block, axis_name, pairs))
    swap = [(i, i ^ 1) for i in range(size)]
    partner = [lax.ppermute(piece, axis_name, swap) for piece in same_core]
    return jnp.stack([jnp.stack(same_core), jnp.stack(partner)], axis=1)


def gather_row_blocks(block, axis_name, size):
    positions = size // 2
    i = lax.axis_index(axis_name)
    z = i // 2
    y = i % 2
    row = [block]
    for s in range(1, positions):
        pairs = [(p * 2 + r, ((p - s) % positions) * 2 + r) for p in range(positions) for r in range(2)]
        row.append(lax.ppermute(block, axis_name, pairs))
    other = lax.ppermute(jnp.stack(row), axis_name, [(j, j ^ 1) for j in range(size)])
    out = []
    for s in range(positions):
        out.append((((z + s) % positions) * 2 + y, row[s]))
        out.append((((z + s) % positions) * 2 + 1 - y, other[s]))
    return out


def all_sum_once(value, axis_name, size):
    pieces = gather_shifted(value, axis_name, size)
    stacked = jnp.roll(jnp.stack(pieces), lax.axis_index(axis_name), axis=0)
    total = stacked[0]
    for j in range(1, size):
        total = total + stacked[j]
    return total


def all_sum(value, axis_name, size):
    step = 1
    while step < size:
        pairs = [(i, i ^ step) for i in range(size)]
        value = value + lax.ppermute(value, axis_name, pairs)
        step *= 2
    return value


def body(travel_time, crossing, bins, transmission, capture):
    tiles = lax.axis_size("tile")
    freqs = lax.axis_size("freq")
    k = lax.axis_index("tile")
    f = lax.axis_index("freq")

    regrouped = lax.all_to_all(travel_time, "tile", split_axis=1, concat_axis=0, tiled=True)
    view = gather_columns(regrouped, "freq", freqs)
    view = jnp.moveaxis(view.reshape((freqs,) + regrouped.shape), 0, 2)
    elements, row_count, _, width = view.shape
    voxels = row_count * freqs * width

    scaled = TWO_PI * bins[0].astype(jnp.float32)
    angle = scaled * view.reshape(elements, voxels)
    field_real = jnp.cos(angle).astype(jnp.bfloat16)
    field_imag = (-jnp.sin(angle)).astype(jnp.bfloat16)
    left = jnp.concatenate([field_real, field_imag], axis=1)
    right = jnp.concatenate([-field_imag, field_real], axis=1)

    positions = tiles // 2
    z = k // 2
    y = k % 2
    row = [capture[0]]
    for s in range(1, positions):
        pairs = [(p * 2 + r, ((p - s) % positions) * 2 + r) for p in range(positions) for r in range(2)]
        row.append(lax.ppermute(capture[0], "tile", pairs))
    swap = [(j, j ^ 1) for j in range(tiles)]
    other = jnp.stack([lax.ppermute(piece, "tile", swap) for piece in row])
    row = jnp.stack(row)

    def partial_focus(group, which_row):
        own = group.shape[2]
        cap_real = group[:, 0].reshape(-1, group.shape[-1])
        cap_imag = group[:, 1].reshape(-1, group.shape[-1])
        product = jnp.dot(cap_real, left, preferred_element_type=jnp.float32) + jnp.dot(
            cap_imag, right, preferred_element_type=jnp.float32
        )
        w_real = product[:, :voxels]
        w_imag = product[:, voxels:]

        def rows_of(field):
            grid = field.reshape(positions, 2, own, voxels)
            picked = lax.dynamic_index_in_dim(grid, which_row, 1, keepdims=False)
            picked = jnp.roll(picked, -z, axis=0)
            return picked.reshape(-1, voxels).astype(jnp.float32)

        g_real = rows_of(field_real)
        g_imag = rows_of(field_imag)
        part_real = jnp.sum(g_real * w_real - g_imag * w_imag, axis=0)
        part_imag = jnp.sum(g_real * w_imag + g_imag * w_real, axis=0)
        return part_real, part_imag

    mine_real, mine_imag = partial_focus(row, y)
    mine_real, mine_imag, other = lax.optimization_barrier((mine_real, mine_imag, other))
    theirs_real, theirs_imag = partial_focus(other, 1 - y)
    focus_real = mine_real + theirs_real
    focus_imag = mine_imag + theirs_imag

    outer = freqs // 2
    focus = jnp.stack([focus_real, focus_imag]).reshape(2, row_count, outer, 2, width)
    focus = jnp.roll(focus, f % 2, axis=3)
    focus = jnp.roll(focus, f // 2, axis=2).reshape(2, row_count, freqs * width)
    focus_real = focus[0]
    focus_imag = focus[1]

    cells = transmission.shape[2]
    match = crossing[None] == lax.broadcasted_iota(jnp.int32, (cells, 1, 1), 0)
    coeff_real = jnp.sum(jnp.where(match, transmission[0, 0][:, None, None], jnp.float32(0.0)), axis=0)
    coeff_imag = jnp.sum(jnp.where(match, transmission[0, 1][:, None, None], jnp.float32(0.0)), axis=0)
    square_real = coeff_real * coeff_real - coeff_imag * coeff_imag
    square_imag = 2.0 * coeff_real * coeff_imag
    part_real = square_real * focus_real - square_imag * focus_imag
    part_imag = square_real * focus_imag + square_imag * focus_real
    partial_image = jnp.stack([part_real, part_imag])
    return all_sum_once(partial_image, "freq", freqs)


def solution(mesh):
    in_specs = (
        P("tile", None, "freq"),
        P("tile", None),
        P("freq"),
        P("freq", None, None),
        P("freq", None, "tile", None),
    )
    out_specs = P(None, "tile", None)
    return jax.shard_map(body, mesh=mesh, in_specs=in_specs, out_specs=out_specs, check_vma=False)
```

```python
import math

import jax
import jax.numpy as jnp
from jax import lax
from jax.sharding import PartitionSpec as P

TWO_PI = 2.0 * math.pi


def gather_shifted(block, axis_name, size):
    pieces = [block]
    for s in range(1, size):
        pairs = [(i, (i - s) % size) for i in range(size)]
        pieces.append(lax.ppermute(block, axis_name, pairs))
    return pieces


def chain(block, axis_name, size, stride, step, direction):
    positions = size // stride
    pairs = []
    for z in range(positions):
        target = z + direction
        if 0 <= target < positions and 0 <= z - direction * (step - 1) < positions:
            pairs += [(z * stride + y, target * stride + y) for y in range(stride)]
    return lax.ppermute(block, axis_name, pairs)


def line_gather(block, axis_name, size):
    positions = size // 2
    z = lax.axis_index(axis_name) // 2
    left = [block]
    right = [block]
    for j in range(1, positions):
        left.append(chain(left[-1], axis_name, size, 2, j, 1))
        right.append(chain(right[-1], axis_name, size, 2, j, -1))
    slots = left[:0:-1] + [block] + right[1:]
    return slots, z


def pair_swap(slots, axis_name, size):
    positions = size // 2
    centre = positions - 1
    out = []
    for i, piece in enumerate(slots):
        d = i - centre
        pairs = [(p * 2 + y, p * 2 + 1 - y) for p in range(positions) if 0 <= p + d < positions for y in range(2)]
        out.append(lax.ppermute(piece, axis_name, pairs))
    return out


def gather_rows(block, axis_name, size):
    positions = size // 2
    slots, z = line_gather(block, axis_name, size)
    other = pair_swap(slots, axis_name, size)
    mine = lax.dynamic_slice_in_dim(jnp.stack(slots), positions - 1 - z, positions, 0)
    theirs = lax.dynamic_slice_in_dim(jnp.stack(other), positions - 1 - z, positions, 0)
    both = jnp.stack([mine, theirs], axis=1)
    both = jnp.roll(both, lax.axis_index(axis_name) % 2, axis=1)
    return both.reshape((size,) + block.shape)


def gather_columns(block, axis_name, size):
    outer = size // 2
    same_core = [block]
    for s in range(1, outer):
        pairs = [(i, (i - 2 * s) % size) for i in range(size)]
        same_core.append(lax.ppermute(block, axis_name, pairs))
    swap = [(i, i ^ 1) for i in range(size)]
    partner = [lax.ppermute(piece, axis_name, swap) for piece in same_core]
    return jnp.stack([jnp.stack(same_core), jnp.stack(partner)], axis=1)


def gather_row_blocks(block, axis_name, size):
    positions = size // 2
    i = lax.axis_index(axis_name)
    z = i // 2
    y = i % 2
    row = [block]
    for s in range(1, positions):
        pairs = [(p * 2 + r, ((p - s) % positions) * 2 + r) for p in range(positions) for r in range(2)]
        row.append(lax.ppermute(block, axis_name, pairs))
    other = lax.ppermute(jnp.stack(row), axis_name, [(j, j ^ 1) for j in range(size)])
    out = []
    for s in range(positions):
        out.append((((z + s) % positions) * 2 + y, row[s]))
        out.append((((z + s) % positions) * 2 + 1 - y, other[s]))
    return out


def all_sum_once(value, axis_name, size):
    pieces = gather_shifted(value, axis_name, size)
    stacked = jnp.roll(jnp.stack(pieces), lax.axis_index(axis_name), axis=0)
    total = stacked[0]
    for j in range(1, size):
        total = total + stacked[j]
    return total


def all_sum(value, axis_name, size):
    step = 1
    while step < size:
        pairs = [(i, i ^ step) for i in range(size)]
        value = value + lax.ppermute(value, axis_name, pairs)
        step *= 2
    return value


def body(travel_time, crossing, bins, transmission, capture):
    tiles = lax.axis_size("tile")
    freqs = lax.axis_size("freq")
    k = lax.axis_index("tile")
    f = lax.axis_index("freq")

    regrouped = lax.all_to_all(travel_time, "tile", split_axis=1, concat_axis=0, tiled=True)
    view = gather_columns(regrouped, "freq", freqs)
    view = jnp.moveaxis(view.reshape((freqs,) + regrouped.shape), 0, 2)
    elements, row_count, _, width = view.shape
    voxels = row_count * freqs * width

    scaled = TWO_PI * bins[0].astype(jnp.float32)
    angle = scaled * view.reshape(elements, voxels)
    field_real = jnp.cos(angle).astype(jnp.bfloat16)
    field_imag = (-jnp.sin(angle)).astype(jnp.bfloat16)
    left = jnp.concatenate([field_real, field_imag], axis=1)
    right = jnp.concatenate([-field_imag, field_real], axis=1)

    positions = tiles // 2
    z = k // 2
    y = k % 2
    own = capture.shape[2]
    swap = [(j, j ^ 1) for j in range(tiles)]
    own_swapped = lax.ppermute(capture[0], "tile", swap)
    shifted = []
    for s in range(1, positions):
        pairs = [(p * 2 + r, ((p - s) % positions) * 2 + r) for p in range(positions) for r in range(2)]
        shifted.append(lax.ppermute(capture[0], "tile", pairs))

    def rows_of(field, which_row):
        grid = field.reshape(positions, 2, own, voxels)
        picked = lax.dynamic_index_in_dim(grid, which_row, 1, keepdims=False)
        return jnp.roll(picked, -z, axis=0).reshape(-1, voxels)

    rows = (rows_of(field_real, y), rows_of(field_imag, y), rows_of(field_real, 1 - y), rows_of(field_imag, 1 - y))
    (left, right, rows), shifted = lax.optimization_barrier(((left, right, rows), shifted))
    other = jnp.stack([own_swapped] + [lax.ppermute(piece, "tile", swap) for piece in shifted])
    row = jnp.stack([capture[0]] + shifted)

    def partial_focus(group, g_real, g_imag):
        cap_real = group[:, 0].reshape(-1, group.shape[-1])
        cap_imag = group[:, 1].reshape(-1, group.shape[-1])
        product = jnp.dot(cap_real, left, preferred_element_type=jnp.float32) + jnp.dot(
            cap_imag, right, preferred_element_type=jnp.float32
        )
        w_real = product[:, :voxels]
        w_imag = product[:, voxels:]
        g_real = g_real.astype(jnp.float32)
        g_imag = g_imag.astype(jnp.float32)
        part_real = jnp.sum(g_real * w_real - g_imag * w_imag, axis=0)
        part_imag = jnp.sum(g_real * w_imag + g_imag * w_real, axis=0)
        return part_real, part_imag

    mine_real, mine_imag = partial_focus(row, rows[0], rows[1])
    mine_real, mine_imag, other = lax.optimization_barrier((mine_real, mine_imag, other))
    theirs_real, theirs_imag = partial_focus(other, rows[2], rows[3])
    focus_real = mine_real + theirs_real
    focus_imag = mine_imag + theirs_imag

    outer = freqs // 2
    focus = jnp.stack([focus_real, focus_imag]).reshape(2, row_count, outer, 2, width)
    focus = jnp.roll(focus, f % 2, axis=3)
    focus = jnp.roll(focus, f // 2, axis=2).reshape(2, row_count, freqs * width)
    focus_real = focus[0]
    focus_imag = focus[1]

    cells = transmission.shape[2]
    match = crossing[None] == lax.broadcasted_iota(jnp.int32, (cells, 1, 1), 0)
    coeff_real = jnp.sum(jnp.where(match, transmission[0, 0][:, None, None], jnp.float32(0.0)), axis=0)
    coeff_imag = jnp.sum(jnp.where(match, transmission[0, 1][:, None, None], jnp.float32(0.0)), axis=0)
    square_real = coeff_real * coeff_real - coeff_imag * coeff_imag
    square_imag = 2.0 * coeff_real * coeff_imag
    part_real = square_real * focus_real - square_imag * focus_imag
    part_imag = square_real * focus_imag + square_imag * focus_real
    partial_image = jnp.stack([part_real, part_imag])
    return all_sum_once(partial_image, "freq", freqs)


def solution(mesh):
    in_specs = (
        P("tile", None, "freq"),
        P("tile", None),
        P("freq"),
        P("freq", None, None),
        P("freq", None, "tile", None),
    )
    out_specs = P(None, "tile", None)
    return jax.shard_map(body, mesh=mesh, in_specs=in_specs, out_specs=out_specs, check_vma=False)
```

```python
import math

import jax
import jax.numpy as jnp
from jax import lax
from jax.sharding import PartitionSpec as P

TWO_PI = 2.0 * math.pi


def gather_shifted(block, axis_name, size):
    pieces = [block]
    for s in range(1, size):
        pairs = [(i, (i - s) % size) for i in range(size)]
        pieces.append(lax.ppermute(block, axis_name, pairs))
    return pieces


def chain(block, axis_name, size, stride, step, direction):
    positions = size // stride
    pairs = []
    for z in range(positions):
        target = z + direction
        if 0 <= target < positions and 0 <= z - direction * (step - 1) < positions:
            pairs += [(z * stride + y, target * stride + y) for y in range(stride)]
    return lax.ppermute(block, axis_name, pairs)


def line_gather(block, axis_name, size):
    positions = size // 2
    z = lax.axis_index(axis_name) // 2
    left = [block]
    right = [block]
    for j in range(1, positions):
        left.append(chain(left[-1], axis_name, size, 2, j, 1))
        right.append(chain(right[-1], axis_name, size, 2, j, -1))
    slots = left[:0:-1] + [block] + right[1:]
    return slots, z


def pair_swap(slots, axis_name, size):
    positions = size // 2
    centre = positions - 1
    out = []
    for i, piece in enumerate(slots):
        d = i - centre
        pairs = [(p * 2 + y, p * 2 + 1 - y) for p in range(positions) if 0 <= p + d < positions for y in range(2)]
        out.append(lax.ppermute(piece, axis_name, pairs))
    return out


def gather_rows(block, axis_name, size):
    positions = size // 2
    slots, z = line_gather(block, axis_name, size)
    other = pair_swap(slots, axis_name, size)
    mine = lax.dynamic_slice_in_dim(jnp.stack(slots), positions - 1 - z, positions, 0)
    theirs = lax.dynamic_slice_in_dim(jnp.stack(other), positions - 1 - z, positions, 0)
    both = jnp.stack([mine, theirs], axis=1)
    both = jnp.roll(both, lax.axis_index(axis_name) % 2, axis=1)
    return both.reshape((size,) + block.shape)


def gather_columns(block, axis_name, size):
    outer = size // 2
    same_core = [block]
    for s in range(1, outer):
        pairs = [(i, (i - 2 * s) % size) for i in range(size)]
        same_core.append(lax.ppermute(block, axis_name, pairs))
    swap = [(i, i ^ 1) for i in range(size)]
    partner = [lax.ppermute(piece, axis_name, swap) for piece in same_core]
    return jnp.stack([jnp.stack(same_core), jnp.stack(partner)], axis=1)


def gather_row_blocks(block, axis_name, size):
    positions = size // 2
    i = lax.axis_index(axis_name)
    z = i // 2
    y = i % 2
    row = [block]
    for s in range(1, positions):
        pairs = [(p * 2 + r, ((p - s) % positions) * 2 + r) for p in range(positions) for r in range(2)]
        row.append(lax.ppermute(block, axis_name, pairs))
    other = lax.ppermute(jnp.stack(row), axis_name, [(j, j ^ 1) for j in range(size)])
    out = []
    for s in range(positions):
        out.append((((z + s) % positions) * 2 + y, row[s]))
        out.append((((z + s) % positions) * 2 + 1 - y, other[s]))
    return out


def all_sum_once(value, axis_name, size):
    pieces = gather_shifted(value, axis_name, size)
    stacked = jnp.roll(jnp.stack(pieces), lax.axis_index(axis_name), axis=0)
    total = stacked[0]
    for j in range(1, size):
        total = total + stacked[j]
    return total


def all_sum(value, axis_name, size):
    step = 1
    while step < size:
        pairs = [(i, i ^ step) for i in range(size)]
        value = value + lax.ppermute(value, axis_name, pairs)
        step *= 2
    return value


def body(travel_time, crossing, bins, transmission, capture):
    tiles = lax.axis_size("tile")
    freqs = lax.axis_size("freq")
    k = lax.axis_index("tile")
    f = lax.axis_index("freq")

    positions = tiles // 2
    z = k // 2
    y = k % 2
    swap = [(j, j ^ 1) for j in range(tiles)]
    row = [capture[0]]
    for s in range(1, positions):
        pairs = [(p * 2 + r, ((p - s) % positions) * 2 + r) for p in range(positions) for r in range(2)]
        row.append(lax.ppermute(capture[0], "tile", pairs))
    own_swapped = lax.ppermute(capture[0], "tile", swap)
    travel_time, own_swapped = lax.optimization_barrier((travel_time, own_swapped))

    regrouped = lax.all_to_all(travel_time, "tile", split_axis=1, concat_axis=0, tiled=True)
    view = gather_columns(regrouped, "freq", freqs)
    view = jnp.moveaxis(view.reshape((freqs,) + regrouped.shape), 0, 2)
    elements, row_count, _, width = view.shape
    voxels = row_count * freqs * width

    scaled = TWO_PI * bins[0].astype(jnp.float32)
    angle = scaled * view.reshape(elements, voxels)
    field_real = jnp.cos(angle).astype(jnp.bfloat16)
    field_imag = (-jnp.sin(angle)).astype(jnp.bfloat16)
    left = jnp.concatenate([field_real, field_imag], axis=1)
    right = jnp.concatenate([-field_imag, field_real], axis=1)

    other = jnp.stack([own_swapped] + [lax.ppermute(piece, "tile", swap) for piece in row[1:]])
    row = jnp.stack(row)

    def partial_focus(group, which_row):
        own = group.shape[2]
        cap_real = group[:, 0].reshape(-1, group.shape[-1])
        cap_imag = group[:, 1].reshape(-1, group.shape[-1])
        product = jnp.dot(cap_real, left, preferred_element_type=jnp.float32) + jnp.dot(
            cap_imag, right, preferred_element_type=jnp.float32
        )
        w_real = product[:, :voxels]
        w_imag = product[:, voxels:]

        def rows_of(field):
            grid = field.reshape(positions, 2, own, voxels)
            picked = lax.dynamic_index_in_dim(grid, which_row, 1, keepdims=False)
            picked = jnp.roll(picked, -z, axis=0)
            return picked.reshape(-1, voxels).astype(jnp.float32)

        g_real = rows_of(field_real)
        g_imag = rows_of(field_imag)
        part_real = jnp.sum(g_real * w_real - g_imag * w_imag, axis=0)
        part_imag = jnp.sum(g_real * w_imag + g_imag * w_real, axis=0)
        return part_real, part_imag

    mine_real, mine_imag = partial_focus(row, y)
    mine_real, mine_imag, other = lax.optimization_barrier((mine_real, mine_imag, other))
    theirs_real, theirs_imag = partial_focus(other, 1 - y)
    focus_real = mine_real + theirs_real
    focus_imag = mine_imag + theirs_imag

    outer = freqs // 2
    focus = jnp.stack([focus_real, focus_imag]).reshape(2, row_count, outer, 2, width)
    focus = jnp.roll(focus, f % 2, axis=3)
    focus = jnp.roll(focus, f // 2, axis=2).reshape(2, row_count, freqs * width)
    focus_real = focus[0]
    focus_imag = focus[1]

    cells = transmission.shape[2]
    match = crossing[None] == lax.broadcasted_iota(jnp.int32, (cells, 1, 1), 0)
    coeff_real = jnp.sum(jnp.where(match, transmission[0, 0][:, None, None], jnp.float32(0.0)), axis=0)
    coeff_imag = jnp.sum(jnp.where(match, transmission[0, 1][:, None, None], jnp.float32(0.0)), axis=0)
    square_real = coeff_real * coeff_real - coeff_imag * coeff_imag
    square_imag = 2.0 * coeff_real * coeff_imag
    part_real = square_real * focus_real - square_imag * focus_imag
    part_imag = square_real * focus_imag + square_imag * focus_real
    partial_image = jnp.stack([part_real, part_imag])
    return all_sum_once(partial_image, "freq", freqs)


def solution(mesh):
    in_specs = (
        P("tile", None, "freq"),
        P("tile", None),
        P("freq"),
        P("freq", None, None),
        P("freq", None, "tile", None),
    )
    out_specs = P(None, "tile", None)
    return jax.shard_map(body, mesh=mesh, in_specs=in_specs, out_specs=out_specs, check_vma=False)
```

```python
import math

import jax
import jax.numpy as jnp
from jax import lax
from jax.sharding import PartitionSpec as P

TWO_PI = 2.0 * math.pi


def gather_shifted(block, axis_name, size):
    pieces = [block]
    for s in range(1, size):
        pairs = [(i, (i - s) % size) for i in range(size)]
        pieces.append(lax.ppermute(block, axis_name, pairs))
    return pieces


def chain(block, axis_name, size, stride, step, direction):
    positions = size // stride
    pairs = []
    for z in range(positions):
        target = z + direction
        if 0 <= target < positions and 0 <= z - direction * (step - 1) < positions:
            pairs += [(z * stride + y, target * stride + y) for y in range(stride)]
    return lax.ppermute(block, axis_name, pairs)


def line_gather(block, axis_name, size):
    positions = size // 2
    z = lax.axis_index(axis_name) // 2
    left = [block]
    right = [block]
    for j in range(1, positions):
        left.append(chain(left[-1], axis_name, size, 2, j, 1))
        right.append(chain(right[-1], axis_name, size, 2, j, -1))
    slots = left[:0:-1] + [block] + right[1:]
    return slots, z


def pair_swap(slots, axis_name, size):
    positions = size // 2
    centre = positions - 1
    out = []
    for i, piece in enumerate(slots):
        d = i - centre
        pairs = [(p * 2 + y, p * 2 + 1 - y) for p in range(positions) if 0 <= p + d < positions for y in range(2)]
        out.append(lax.ppermute(piece, axis_name, pairs))
    return out


def gather_rows(block, axis_name, size):
    positions = size // 2
    slots, z = line_gather(block, axis_name, size)
    other = pair_swap(slots, axis_name, size)
    mine = lax.dynamic_slice_in_dim(jnp.stack(slots), positions - 1 - z, positions, 0)
    theirs = lax.dynamic_slice_in_dim(jnp.stack(other), positions - 1 - z, positions, 0)
    both = jnp.stack([mine, theirs], axis=1)
    both = jnp.roll(both, lax.axis_index(axis_name) % 2, axis=1)
    return both.reshape((size,) + block.shape)


def gather_columns(block, axis_name, size):
    outer = size // 2
    same_core = [block]
    for s in range(1, outer):
        pairs = [(i, (i - 2 * s) % size) for i in range(size)]
        same_core.append(lax.ppermute(block, axis_name, pairs))
    swap = [(i, i ^ 1) for i in range(size)]
    partner = [lax.ppermute(piece, axis_name, swap) for piece in same_core]
    return jnp.stack([jnp.stack(same_core), jnp.stack(partner)], axis=1)


def gather_row_blocks(block, axis_name, size):
    positions = size // 2
    i = lax.axis_index(axis_name)
    z = i // 2
    y = i % 2
    row = [block]
    for s in range(1, positions):
        pairs = [(p * 2 + r, ((p - s) % positions) * 2 + r) for p in range(positions) for r in range(2)]
        row.append(lax.ppermute(block, axis_name, pairs))
    other = lax.ppermute(jnp.stack(row), axis_name, [(j, j ^ 1) for j in range(size)])
    out = []
    for s in range(positions):
        out.append((((z + s) % positions) * 2 + y, row[s]))
        out.append((((z + s) % positions) * 2 + 1 - y, other[s]))
    return out


def all_sum_once(value, axis_name, size):
    pieces = gather_shifted(value, axis_name, size)
    stacked = jnp.roll(jnp.stack(pieces), lax.axis_index(axis_name), axis=0)
    total = stacked[0]
    for j in range(1, size):
        total = total + stacked[j]
    return total


def all_sum(value, axis_name, size):
    step = 1
    while step < size:
        pairs = [(i, i ^ step) for i in range(size)]
        value = value + lax.ppermute(value, axis_name, pairs)
        step *= 2
    return value


def body(travel_time, crossing, bins, transmission, capture):
    tiles = lax.axis_size("tile")
    freqs = lax.axis_size("freq")
    k = lax.axis_index("tile")
    f = lax.axis_index("freq")

    positions = tiles // 2
    z = k // 2
    y = k % 2
    per_tile = travel_time.shape[1] // tiles
    pieces = [lax.dynamic_slice_in_dim(travel_time, 2 * z * per_tile, 2 * per_tile, 1)]
    for s in range(1, positions):
        target = (z - s) % positions
        sent = lax.dynamic_slice_in_dim(travel_time, 2 * target * per_tile, 2 * per_tile, 1)
        pairs = [(p * 2 + r, ((p - s) % positions) * 2 + r) for p in range(positions) for r in range(2)]
        pieces.append(lax.ppermute(sent, "tile", pairs))
    pieces = jnp.stack(pieces)
    mine_tt = lax.dynamic_slice_in_dim(pieces, y * per_tile, per_tile, 2)
    theirs_tt = lax.ppermute(
        lax.dynamic_slice_in_dim(pieces, (1 - y) * per_tile, per_tile, 2), "tile", [(j, j ^ 1) for j in range(tiles)]
    )
    both_tt = jnp.stack([mine_tt, theirs_tt], axis=1)
    both_tt = jnp.roll(jnp.roll(both_tt, z, axis=0), y, axis=1)
    regrouped = both_tt.reshape((-1,) + both_tt.shape[3:])
    view = gather_columns(regrouped, "freq", freqs)
    view = jnp.moveaxis(view.reshape((freqs,) + regrouped.shape), 0, 2)
    elements, row_count, _, width = view.shape
    voxels = row_count * freqs * width

    scaled = TWO_PI * bins[0].astype(jnp.float32)
    angle = scaled * view.reshape(elements, voxels)
    field_real = jnp.cos(angle).astype(jnp.bfloat16)
    field_imag = (-jnp.sin(angle)).astype(jnp.bfloat16)
    left = jnp.concatenate([field_real, field_imag], axis=1)
    right = jnp.concatenate([-field_imag, field_real], axis=1)

    row = [capture[0]]
    for s in range(1, positions):
        pairs = [(p * 2 + r, ((p - s) % positions) * 2 + r) for p in range(positions) for r in range(2)]
        row.append(lax.ppermute(capture[0], "tile", pairs))
    row = jnp.stack(row)
    other = lax.ppermute(row, "tile", [(j, j ^ 1) for j in range(tiles)])

    def partial_focus(group, which_row):
        own = group.shape[2]
        cap_real = group[:, 0].reshape(-1, group.shape[-1])
        cap_imag = group[:, 1].reshape(-1, group.shape[-1])
        product = jnp.dot(cap_real, left, preferred_element_type=jnp.float32) + jnp.dot(
            cap_imag, right, preferred_element_type=jnp.float32
        )
        w_real = product[:, :voxels]
        w_imag = product[:, voxels:]

        def rows_of(field):
            grid = field.reshape(positions, 2, own, voxels)
            picked = lax.dynamic_index_in_dim(grid, which_row, 1, keepdims=False)
            picked = jnp.roll(picked, -z, axis=0)
            return picked.reshape(-1, voxels).astype(jnp.float32)

        g_real = rows_of(field_real)
        g_imag = rows_of(field_imag)
        part_real = jnp.sum(g_real * w_real - g_imag * w_imag, axis=0)
        part_imag = jnp.sum(g_real * w_imag + g_imag * w_real, axis=0)
        return part_real, part_imag

    mine_real, mine_imag = partial_focus(row, y)
    mine_real, mine_imag, other = lax.optimization_barrier((mine_real, mine_imag, other))
    theirs_real, theirs_imag = partial_focus(other, 1 - y)
    focus_real = mine_real + theirs_real
    focus_imag = mine_imag + theirs_imag

    outer = freqs // 2
    focus = jnp.stack([focus_real, focus_imag]).reshape(2, row_count, outer, 2, width)
    focus = jnp.roll(focus, f % 2, axis=3)
    focus = jnp.roll(focus, f // 2, axis=2).reshape(2, row_count, freqs * width)
    focus_real = focus[0]
    focus_imag = focus[1]

    cells = transmission.shape[2]
    match = crossing[None] == lax.broadcasted_iota(jnp.int32, (cells, 1, 1), 0)
    coeff_real = jnp.sum(jnp.where(match, transmission[0, 0][:, None, None], jnp.float32(0.0)), axis=0)
    coeff_imag = jnp.sum(jnp.where(match, transmission[0, 1][:, None, None], jnp.float32(0.0)), axis=0)
    square_real = coeff_real * coeff_real - coeff_imag * coeff_imag
    square_imag = 2.0 * coeff_real * coeff_imag
    part_real = square_real * focus_real - square_imag * focus_imag
    part_imag = square_real * focus_imag + square_imag * focus_real
    partial_image = jnp.stack([part_real, part_imag])
    return all_sum_once(partial_image, "freq", freqs)


def solution(mesh):
    in_specs = (
        P("tile", None, "freq"),
        P("tile", None),
        P("freq"),
        P("freq", None, None),
        P("freq", None, "tile", None),
    )
    out_specs = P(None, "tile", None)
    return jax.shard_map(body, mesh=mesh, in_specs=in_specs, out_specs=out_specs, check_vma=False)
```

```python
import math

import jax
import jax.numpy as jnp
from jax import lax
from jax.sharding import PartitionSpec as P

TWO_PI = 2.0 * math.pi


def gather_shifted(block, axis_name, size):
    pieces = [block]
    for s in range(1, size):
        pairs = [(i, (i - s) % size) for i in range(size)]
        pieces.append(lax.ppermute(block, axis_name, pairs))
    return pieces


def chain(block, axis_name, size, stride, step, direction):
    positions = size // stride
    pairs = []
    for z in range(positions):
        target = z + direction
        if 0 <= target < positions and 0 <= z - direction * (step - 1) < positions:
            pairs += [(z * stride + y, target * stride + y) for y in range(stride)]
    return lax.ppermute(block, axis_name, pairs)


def line_gather(block, axis_name, size):
    positions = size // 2
    z = lax.axis_index(axis_name) // 2
    left = [block]
    right = [block]
    for j in range(1, positions):
        left.append(chain(left[-1], axis_name, size, 2, j, 1))
        right.append(chain(right[-1], axis_name, size, 2, j, -1))
    slots = left[:0:-1] + [block] + right[1:]
    return slots, z


def pair_swap(slots, axis_name, size):
    positions = size // 2
    centre = positions - 1
    out = []
    for i, piece in enumerate(slots):
        d = i - centre
        pairs = [(p * 2 + y, p * 2 + 1 - y) for p in range(positions) if 0 <= p + d < positions for y in range(2)]
        out.append(lax.ppermute(piece, axis_name, pairs))
    return out


def gather_rows(block, axis_name, size):
    positions = size // 2
    slots, z = line_gather(block, axis_name, size)
    other = pair_swap(slots, axis_name, size)
    mine = lax.dynamic_slice_in_dim(jnp.stack(slots), positions - 1 - z, positions, 0)
    theirs = lax.dynamic_slice_in_dim(jnp.stack(other), positions - 1 - z, positions, 0)
    both = jnp.stack([mine, theirs], axis=1)
    both = jnp.roll(both, lax.axis_index(axis_name) % 2, axis=1)
    return both.reshape((size,) + block.shape)


def gather_columns(block, axis_name, size):
    outer = size // 2
    same_core = [block]
    for s in range(1, outer):
        pairs = [(i, (i - 2 * s) % size) for i in range(size)]
        same_core.append(lax.ppermute(block, axis_name, pairs))
    swap = [(i, i ^ 1) for i in range(size)]
    partner = [lax.ppermute(piece, axis_name, swap) for piece in same_core]
    return jnp.stack([jnp.stack(same_core), jnp.stack(partner)], axis=1)


def gather_row_blocks(block, axis_name, size):
    positions = size // 2
    i = lax.axis_index(axis_name)
    z = i // 2
    y = i % 2
    row = [block]
    for s in range(1, positions):
        pairs = [(p * 2 + r, ((p - s) % positions) * 2 + r) for p in range(positions) for r in range(2)]
        row.append(lax.ppermute(block, axis_name, pairs))
    other = lax.ppermute(jnp.stack(row), axis_name, [(j, j ^ 1) for j in range(size)])
    out = []
    for s in range(positions):
        out.append((((z + s) % positions) * 2 + y, row[s]))
        out.append((((z + s) % positions) * 2 + 1 - y, other[s]))
    return out


def all_sum_once(value, axis_name, size):
    pieces = gather_shifted(value, axis_name, size)
    stacked = jnp.roll(jnp.stack(pieces), lax.axis_index(axis_name), axis=0)
    total = stacked[0]
    for j in range(1, size):
        total = total + stacked[j]
    return total


def all_sum(value, axis_name, size):
    step = 1
    while step < size:
        pairs = [(i, i ^ step) for i in range(size)]
        value = value + lax.ppermute(value, axis_name, pairs)
        step *= 2
    return value


def body(travel_time, crossing, bins, transmission, capture):
    tiles = lax.axis_size("tile")
    freqs = lax.axis_size("freq")
    k = lax.axis_index("tile")
    f = lax.axis_index("freq")

    positions = tiles // 2
    z = k // 2
    y = k % 2
    swap = [(j, j ^ 1) for j in range(tiles)]

    cap_row = [capture[0]]
    for s in range(1, positions):
        pairs = [(p * 2 + r, ((p - s) % positions) * 2 + r) for p in range(positions) for r in range(2)]
        cap_row.append(lax.ppermute(capture[0], "tile", pairs))
    own_swapped = lax.ppermute(capture[0], "tile", swap)

    per_tile = travel_time.shape[1] // tiles
    pieces = [lax.dynamic_slice_in_dim(travel_time, 2 * z * per_tile, 2 * per_tile, 1)]
    for s in range(1, positions):
        target = (z - s) % positions
        sent = lax.dynamic_slice_in_dim(travel_time, 2 * target * per_tile, 2 * per_tile, 1)
        pairs = [(p * 2 + r, ((p - s) % positions) * 2 + r) for p in range(positions) for r in range(2)]
        pieces.append(lax.ppermute(sent, "tile", pairs))
    pieces = jnp.stack(pieces)
    mine_tt = lax.dynamic_slice_in_dim(pieces, y * per_tile, per_tile, 2)
    theirs_tt = lax.ppermute(
        lax.dynamic_slice_in_dim(pieces, (1 - y) * per_tile, per_tile, 2), "tile", [(j, j ^ 1) for j in range(tiles)]
    )
    both_tt = jnp.stack([mine_tt, theirs_tt], axis=1)
    both_tt = jnp.roll(jnp.roll(both_tt, z, axis=0), y, axis=1)
    regrouped = both_tt.reshape((-1,) + both_tt.shape[3:])
    view = gather_columns(regrouped, "freq", freqs)
    view = jnp.moveaxis(view.reshape((freqs,) + regrouped.shape), 0, 2)
    elements, row_count, _, width = view.shape
    voxels = row_count * freqs * width

    scaled = TWO_PI * bins[0].astype(jnp.float32)
    angle = scaled * view.reshape(elements, voxels)
    field_real = jnp.cos(angle).astype(jnp.bfloat16)
    field_imag = (-jnp.sin(angle)).astype(jnp.bfloat16)
    left = jnp.concatenate([field_real, field_imag], axis=1)
    right = jnp.concatenate([-field_imag, field_real], axis=1)

    row = cap_row
    other = (own_swapped, lax.ppermute(jnp.stack(row[1:]), "tile", swap))
    row = jnp.stack(row)
    own = capture.shape[2]

    def rows_of(field, which_row):
        grid = field.reshape(positions, 2, own, voxels)
        picked = lax.dynamic_index_in_dim(grid, which_row, 1, keepdims=False)
        return jnp.roll(picked, -z, axis=0).reshape(-1, voxels)

    def partial_focus(group, g_real, g_imag):
        cap_real = group[:, 0].reshape(-1, group.shape[-1])
        cap_imag = group[:, 1].reshape(-1, group.shape[-1])
        product = jnp.dot(cap_real, left, preferred_element_type=jnp.float32) + jnp.dot(
            cap_imag, right, preferred_element_type=jnp.float32
        )
        w_real = product[:, :voxels]
        w_imag = product[:, voxels:]
        g_real = g_real.astype(jnp.float32)
        g_imag = g_imag.astype(jnp.float32)
        part_real = jnp.sum(g_real * w_real - g_imag * w_imag, axis=0)
        part_imag = jnp.sum(g_real * w_imag + g_imag * w_real, axis=0)
        return part_real, part_imag

    mine_real, mine_imag = partial_focus(row, rows_of(field_real, y), rows_of(field_imag, y))
    theirs_rows = (rows_of(field_real, 1 - y), rows_of(field_imag, 1 - y))
    mine_real, mine_imag, theirs_rows, other = lax.optimization_barrier((mine_real, mine_imag, theirs_rows, other))
    theirs_real, theirs_imag = partial_focus(jnp.concatenate([other[0][None], other[1]]), *theirs_rows)
    focus_real = mine_real + theirs_real
    focus_imag = mine_imag + theirs_imag

    outer = freqs // 2
    focus = jnp.stack([focus_real, focus_imag]).reshape(2, row_count, outer, 2, width)
    focus = jnp.roll(focus, f % 2, axis=3)
    focus = jnp.roll(focus, f // 2, axis=2).reshape(2, row_count, freqs * width)
    focus_real = focus[0]
    focus_imag = focus[1]

    cells = transmission.shape[2]
    match = crossing[None] == lax.broadcasted_iota(jnp.int32, (cells, 1, 1), 0)
    coeff_real = jnp.sum(jnp.where(match, transmission[0, 0][:, None, None], jnp.float32(0.0)), axis=0)
    coeff_imag = jnp.sum(jnp.where(match, transmission[0, 1][:, None, None], jnp.float32(0.0)), axis=0)
    square_real = coeff_real * coeff_real - coeff_imag * coeff_imag
    square_imag = 2.0 * coeff_real * coeff_imag
    part_real = square_real * focus_real - square_imag * focus_imag
    part_imag = square_real * focus_imag + square_imag * focus_real
    partial_image = jnp.stack([part_real, part_imag])
    return all_sum_once(partial_image, "freq", freqs)


def solution(mesh):
    in_specs = (
        P("tile", None, "freq"),
        P("tile", None),
        P("freq"),
        P("freq", None, None),
        P("freq", None, "tile", None),
    )
    out_specs = P(None, "tile", None)
    return jax.shard_map(body, mesh=mesh, in_specs=in_specs, out_specs=out_specs, check_vma=False)
```

```python
import math

import jax
import jax.numpy as jnp
from jax import lax
from jax.sharding import PartitionSpec as P

TWO_PI = 2.0 * math.pi


def gather_shifted(block, axis_name, size):
    pieces = [block]
    for s in range(1, size):
        pairs = [(i, (i - s) % size) for i in range(size)]
        pieces.append(lax.ppermute(block, axis_name, pairs))
    return pieces


def chain(block, axis_name, size, stride, step, direction):
    positions = size // stride
    pairs = []
    for z in range(positions):
        target = z + direction
        if 0 <= target < positions and 0 <= z - direction * (step - 1) < positions:
            pairs += [(z * stride + y, target * stride + y) for y in range(stride)]
    return lax.ppermute(block, axis_name, pairs)


def line_gather(block, axis_name, size):
    positions = size // 2
    z = lax.axis_index(axis_name) // 2
    left = [block]
    right = [block]
    for j in range(1, positions):
        left.append(chain(left[-1], axis_name, size, 2, j, 1))
        right.append(chain(right[-1], axis_name, size, 2, j, -1))
    slots = left[:0:-1] + [block] + right[1:]
    return slots, z


def pair_swap(slots, axis_name, size):
    positions = size // 2
    centre = positions - 1
    out = []
    for i, piece in enumerate(slots):
        d = i - centre
        pairs = [(p * 2 + y, p * 2 + 1 - y) for p in range(positions) if 0 <= p + d < positions for y in range(2)]
        out.append(lax.ppermute(piece, axis_name, pairs))
    return out


def gather_rows(block, axis_name, size):
    positions = size // 2
    slots, z = line_gather(block, axis_name, size)
    other = pair_swap(slots, axis_name, size)
    mine = lax.dynamic_slice_in_dim(jnp.stack(slots), positions - 1 - z, positions, 0)
    theirs = lax.dynamic_slice_in_dim(jnp.stack(other), positions - 1 - z, positions, 0)
    both = jnp.stack([mine, theirs], axis=1)
    both = jnp.roll(both, lax.axis_index(axis_name) % 2, axis=1)
    return both.reshape((size,) + block.shape)


def gather_columns(block, axis_name, size):
    outer = size // 2
    same_core = [block]
    for s in range(1, outer):
        pairs = [(i, (i - 2 * s) % size) for i in range(size)]
        same_core.append(lax.ppermute(block, axis_name, pairs))
    swap = [(i, i ^ 1) for i in range(size)]
    partner = [lax.ppermute(piece, axis_name, swap) for piece in same_core]
    return jnp.stack([jnp.stack(same_core), jnp.stack(partner)], axis=1)


def gather_row_blocks(block, axis_name, size):
    positions = size // 2
    i = lax.axis_index(axis_name)
    z = i // 2
    y = i % 2
    row = [block]
    for s in range(1, positions):
        pairs = [(p * 2 + r, ((p - s) % positions) * 2 + r) for p in range(positions) for r in range(2)]
        row.append(lax.ppermute(block, axis_name, pairs))
    other = lax.ppermute(jnp.stack(row), axis_name, [(j, j ^ 1) for j in range(size)])
    out = []
    for s in range(positions):
        out.append((((z + s) % positions) * 2 + y, row[s]))
        out.append((((z + s) % positions) * 2 + 1 - y, other[s]))
    return out


def all_sum_once(value, axis_name, size):
    pieces = gather_shifted(value, axis_name, size)
    stacked = jnp.roll(jnp.stack(pieces), lax.axis_index(axis_name), axis=0)
    total = stacked[0]
    for j in range(1, size):
        total = total + stacked[j]
    return total


def all_sum(value, axis_name, size):
    step = 1
    while step < size:
        pairs = [(i, i ^ step) for i in range(size)]
        value = value + lax.ppermute(value, axis_name, pairs)
        step *= 2
    return value


def body(travel_time, crossing, bins, transmission, capture):
    tiles = lax.axis_size("tile")
    freqs = lax.axis_size("freq")
    k = lax.axis_index("tile")
    f = lax.axis_index("freq")

    positions = tiles // 2
    z = k // 2
    y = k % 2
    swap = [(j, j ^ 1) for j in range(tiles)]

    cap_row = [capture[0]]
    for s in range(1, positions):
        pairs = [(p * 2 + r, ((p - s) % positions) * 2 + r) for p in range(positions) for r in range(2)]
        cap_row.append(lax.ppermute(capture[0], "tile", pairs))
    own_swapped = lax.ppermute(capture[0], "tile", swap)

    per_tile = travel_time.shape[1] // tiles
    pieces = [lax.dynamic_slice_in_dim(travel_time, 2 * z * per_tile, 2 * per_tile, 1)]
    for s in range(1, positions):
        target = (z - s) % positions
        sent = lax.dynamic_slice_in_dim(travel_time, 2 * target * per_tile, 2 * per_tile, 1)
        pairs = [(p * 2 + r, ((p - s) % positions) * 2 + r) for p in range(positions) for r in range(2)]
        pieces.append(lax.ppermute(sent, "tile", pairs))
    pieces = jnp.stack(pieces)
    mine_tt = lax.dynamic_slice_in_dim(pieces, y * per_tile, per_tile, 2)
    neighbour_tt = lax.dynamic_slice_in_dim(pieces, (1 - y) * per_tile, per_tile, 2)
    outer = freqs // 2
    same_core = [jnp.stack([mine_tt, lax.ppermute(neighbour_tt, "tile", swap)])]
    for so in range(1, outer):
        straight = [(i, (i - 2 * so) % freqs) for i in range(freqs)]
        diagonal = [
            (i * tiles + t, ((i - 2 * so) % freqs) * tiles + (t ^ 1)) for i in range(freqs) for t in range(tiles)
        ]
        same_core.append(
            jnp.stack(
                [lax.ppermute(mine_tt, "freq", straight), lax.ppermute(neighbour_tt, ("freq", "tile"), diagonal)]
            )
        )
    same_core = jnp.stack(same_core)
    partner = lax.ppermute(same_core, "freq", [(i, i ^ 1) for i in range(freqs)])
    view = jnp.stack([same_core, partner], axis=1)
    view = jnp.transpose(view, (3, 2, 4, 5, 0, 1, 6))
    view = jnp.roll(jnp.roll(view, z, axis=0), y, axis=1)
    view = view.reshape((-1,) + view.shape[3:4] + (freqs,) + view.shape[6:])
    elements, row_count, _, width = view.shape
    voxels = row_count * freqs * width

    scaled = TWO_PI * bins[0].astype(jnp.float32)
    angle = scaled * view.reshape(elements, voxels)
    field_real = jnp.cos(angle).astype(jnp.bfloat16)
    field_imag = (-jnp.sin(angle)).astype(jnp.bfloat16)
    left = jnp.concatenate([field_real, field_imag], axis=1)
    right = jnp.concatenate([-field_imag, field_real], axis=1)

    row = cap_row
    other = (own_swapped, lax.ppermute(jnp.stack(row[1:]), "tile", swap))
    row = jnp.stack(row)
    own = capture.shape[2]

    def rows_of(field, which_row):
        grid = field.reshape(positions, 2, own, voxels)
        picked = lax.dynamic_index_in_dim(grid, which_row, 1, keepdims=False)
        return jnp.roll(picked, -z, axis=0).reshape(-1, voxels)

    def partial_focus(group, g_real, g_imag):
        cap_real = group[:, 0].reshape(-1, group.shape[-1])
        cap_imag = group[:, 1].reshape(-1, group.shape[-1])
        product = jnp.dot(cap_real, left, preferred_element_type=jnp.float32) + jnp.dot(
            cap_imag, right, preferred_element_type=jnp.float32
        )
        w_real = product[:, :voxels]
        w_imag = product[:, voxels:]
        g_real = g_real.astype(jnp.float32)
        g_imag = g_imag.astype(jnp.float32)
        part_real = jnp.sum(g_real * w_real - g_imag * w_imag, axis=0)
        part_imag = jnp.sum(g_real * w_imag + g_imag * w_real, axis=0)
        return part_real, part_imag

    mine_real, mine_imag = partial_focus(row, rows_of(field_real, y), rows_of(field_imag, y))
    theirs_rows = (rows_of(field_real, 1 - y), rows_of(field_imag, 1 - y))
    mine_real, mine_imag, theirs_rows, other = lax.optimization_barrier((mine_real, mine_imag, theirs_rows, other))
    theirs_real, theirs_imag = partial_focus(jnp.concatenate([other[0][None], other[1]]), *theirs_rows)
    focus_real = mine_real + theirs_real
    focus_imag = mine_imag + theirs_imag

    outer = freqs // 2
    focus = jnp.stack([focus_real, focus_imag]).reshape(2, row_count, outer, 2, width)
    focus = jnp.roll(focus, f % 2, axis=3)
    focus = jnp.roll(focus, f // 2, axis=2).reshape(2, row_count, freqs * width)
    focus_real = focus[0]
    focus_imag = focus[1]

    cells = transmission.shape[2]
    match = crossing[None] == lax.broadcasted_iota(jnp.int32, (cells, 1, 1), 0)
    coeff_real = jnp.sum(jnp.where(match, transmission[0, 0][:, None, None], jnp.float32(0.0)), axis=0)
    coeff_imag = jnp.sum(jnp.where(match, transmission[0, 1][:, None, None], jnp.float32(0.0)), axis=0)
    square_real = coeff_real * coeff_real - coeff_imag * coeff_imag
    square_imag = 2.0 * coeff_real * coeff_imag
    part_real = square_real * focus_real - square_imag * focus_imag
    part_imag = square_real * focus_imag + square_imag * focus_real
    partial_image = jnp.stack([part_real, part_imag])
    return all_sum_once(partial_image, "freq", freqs)


def solution(mesh):
    in_specs = (
        P("tile", None, "freq"),
        P("tile", None),
        P("freq"),
        P("freq", None, None),
        P("freq", None, "tile", None),
    )
    out_specs = P(None, "tile", None)
    return jax.shard_map(body, mesh=mesh, in_specs=in_specs, out_specs=out_specs, check_vma=False)
```

```python
import math

import jax
import jax.numpy as jnp
from jax import lax
from jax.sharding import PartitionSpec as P

TWO_PI = 2.0 * math.pi


def gather_shifted(block, axis_name, size):
    pieces = [block]
    for s in range(1, size):
        pairs = [(i, (i - s) % size) for i in range(size)]
        pieces.append(lax.ppermute(block, axis_name, pairs))
    return pieces


def chain(block, axis_name, size, stride, step, direction):
    positions = size // stride
    pairs = []
    for z in range(positions):
        target = z + direction
        if 0 <= target < positions and 0 <= z - direction * (step - 1) < positions:
            pairs += [(z * stride + y, target * stride + y) for y in range(stride)]
    return lax.ppermute(block, axis_name, pairs)


def line_gather(block, axis_name, size):
    positions = size // 2
    z = lax.axis_index(axis_name) // 2
    left = [block]
    right = [block]
    for j in range(1, positions):
        left.append(chain(left[-1], axis_name, size, 2, j, 1))
        right.append(chain(right[-1], axis_name, size, 2, j, -1))
    slots = left[:0:-1] + [block] + right[1:]
    return slots, z


def pair_swap(slots, axis_name, size):
    positions = size // 2
    centre = positions - 1
    out = []
    for i, piece in enumerate(slots):
        d = i - centre
        pairs = [(p * 2 + y, p * 2 + 1 - y) for p in range(positions) if 0 <= p + d < positions for y in range(2)]
        out.append(lax.ppermute(piece, axis_name, pairs))
    return out


def gather_rows(block, axis_name, size):
    positions = size // 2
    slots, z = line_gather(block, axis_name, size)
    other = pair_swap(slots, axis_name, size)
    mine = lax.dynamic_slice_in_dim(jnp.stack(slots), positions - 1 - z, positions, 0)
    theirs = lax.dynamic_slice_in_dim(jnp.stack(other), positions - 1 - z, positions, 0)
    both = jnp.stack([mine, theirs], axis=1)
    both = jnp.roll(both, lax.axis_index(axis_name) % 2, axis=1)
    return both.reshape((size,) + block.shape)


def gather_columns(block, axis_name, size):
    outer = size // 2
    same_core = [block]
    for s in range(1, outer):
        pairs = [(i, (i - 2 * s) % size) for i in range(size)]
        same_core.append(lax.ppermute(block, axis_name, pairs))
    swap = [(i, i ^ 1) for i in range(size)]
    partner = [lax.ppermute(piece, axis_name, swap) for piece in same_core]
    return jnp.stack([jnp.stack(same_core), jnp.stack(partner)], axis=1)


def gather_row_blocks(block, axis_name, size):
    positions = size // 2
    i = lax.axis_index(axis_name)
    z = i // 2
    y = i % 2
    row = [block]
    for s in range(1, positions):
        pairs = [(p * 2 + r, ((p - s) % positions) * 2 + r) for p in range(positions) for r in range(2)]
        row.append(lax.ppermute(block, axis_name, pairs))
    other = lax.ppermute(jnp.stack(row), axis_name, [(j, j ^ 1) for j in range(size)])
    out = []
    for s in range(positions):
        out.append((((z + s) % positions) * 2 + y, row[s]))
        out.append((((z + s) % positions) * 2 + 1 - y, other[s]))
    return out


def all_sum_once(value, axis_name, size):
    pieces = gather_shifted(value, axis_name, size)
    stacked = jnp.roll(jnp.stack(pieces), lax.axis_index(axis_name), axis=0)
    total = stacked[0]
    for j in range(1, size):
        total = total + stacked[j]
    return total


def all_sum(value, axis_name, size):
    step = 1
    while step < size:
        pairs = [(i, i ^ step) for i in range(size)]
        value = value + lax.ppermute(value, axis_name, pairs)
        step *= 2
    return value


def body(travel_time, crossing, bins, transmission, capture):
    tiles = lax.axis_size("tile")
    freqs = lax.axis_size("freq")
    k = lax.axis_index("tile")
    f = lax.axis_index("freq")

    positions = tiles // 2
    z = k // 2
    y = k % 2
    swap = [(j, j ^ 1) for j in range(tiles)]

    local = jnp.transpose(capture[0], (1, 0, 2)).reshape(capture.shape[2], -1)
    cap_row = [local]
    for s in range(1, positions):
        pairs = [(p * 2 + r, ((p - s) % positions) * 2 + r) for p in range(positions) for r in range(2)]
        cap_row.append(lax.ppermute(local, "tile", pairs))
    own_swapped = lax.ppermute(local, "tile", swap)

    per_tile = travel_time.shape[1] // tiles
    pieces = [lax.dynamic_slice_in_dim(travel_time, 2 * z * per_tile, 2 * per_tile, 1)]
    for s in range(1, positions):
        target = (z - s) % positions
        sent = lax.dynamic_slice_in_dim(travel_time, 2 * target * per_tile, 2 * per_tile, 1)
        pairs = [(p * 2 + r, ((p - s) % positions) * 2 + r) for p in range(positions) for r in range(2)]
        pieces.append(lax.ppermute(sent, "tile", pairs))
    pieces = jnp.stack(pieces)
    mine_tt = lax.dynamic_slice_in_dim(pieces, y * per_tile, per_tile, 2)
    theirs_tt = lax.ppermute(
        lax.dynamic_slice_in_dim(pieces, (1 - y) * per_tile, per_tile, 2), "tile", [(j, j ^ 1) for j in range(tiles)]
    )
    both_tt = jnp.stack([mine_tt, theirs_tt], axis=1)
    both_tt = jnp.roll(jnp.roll(both_tt, z, axis=0), y, axis=1)
    regrouped = both_tt.reshape((-1,) + both_tt.shape[3:])
    view = gather_columns(regrouped, "freq", freqs)
    view = jnp.moveaxis(view.reshape((freqs,) + regrouped.shape), 0, 2)
    elements, row_count, _, width = view.shape
    voxels = row_count * freqs * width

    scaled = TWO_PI * bins[0].astype(jnp.float32)
    angle = scaled * view.reshape(elements, voxels)
    field_real = jnp.cos(angle).astype(jnp.bfloat16)
    field_imag = (-jnp.sin(angle)).astype(jnp.bfloat16)
    fields = jnp.concatenate(
        [jnp.concatenate([field_real, field_imag], axis=1), jnp.concatenate([-field_imag, field_real], axis=1)],
        axis=0,
    )

    rest = lax.ppermute(jnp.stack(cap_row[1:]), "tile", swap)
    row = jnp.stack(cap_row)
    own = capture.shape[2]

    def rows_of(field, which_row):
        grid = field.reshape(positions, 2, own, voxels)
        picked = lax.dynamic_index_in_dim(grid, which_row, 1, keepdims=False)
        return jnp.roll(picked, -z, axis=0).reshape(-1, voxels)

    def partial_focus(group, g_real, g_imag):
        product = jnp.dot(group.reshape(-1, group.shape[-1]), fields, preferred_element_type=jnp.float32)
        w_real = product[:, :voxels]
        w_imag = product[:, voxels:]
        g_real = g_real.astype(jnp.float32)
        g_imag = g_imag.astype(jnp.float32)
        part_real = jnp.sum(g_real * w_real - g_imag * w_imag, axis=0)
        part_imag = jnp.sum(g_real * w_imag + g_imag * w_real, axis=0)
        return part_real, part_imag

    theirs_real_rows = rows_of(field_real, 1 - y)
    theirs_imag_rows = rows_of(field_imag, 1 - y)
    mine_real, mine_imag = partial_focus(row, rows_of(field_real, y), rows_of(field_imag, y))
    first_real, first_imag = partial_focus(own_swapped, theirs_real_rows[:own], theirs_imag_rows[:own])
    theirs_rows = (theirs_real_rows[own:], theirs_imag_rows[own:])
    mine_real, mine_imag, first_real, first_imag, theirs_rows, rest = lax.optimization_barrier(
        (mine_real, mine_imag, first_real, first_imag, theirs_rows, rest)
    )
    theirs_real, theirs_imag = partial_focus(rest, *theirs_rows)
    focus_real = mine_real + (first_real + theirs_real)
    focus_imag = mine_imag + (first_imag + theirs_imag)

    outer = freqs // 2
    focus = jnp.stack([focus_real, focus_imag]).reshape(2, row_count, outer, 2, width)
    focus = jnp.roll(focus, f % 2, axis=3)
    focus = jnp.roll(focus, f // 2, axis=2).reshape(2, row_count, freqs * width)
    focus_real = focus[0]
    focus_imag = focus[1]

    cells = transmission.shape[2]
    match = crossing[None] == lax.broadcasted_iota(jnp.int32, (cells, 1, 1), 0)
    coeff_real = jnp.sum(jnp.where(match, transmission[0, 0][:, None, None], jnp.float32(0.0)), axis=0)
    coeff_imag = jnp.sum(jnp.where(match, transmission[0, 1][:, None, None], jnp.float32(0.0)), axis=0)
    square_real = coeff_real * coeff_real - coeff_imag * coeff_imag
    square_imag = 2.0 * coeff_real * coeff_imag
    part_real = square_real * focus_real - square_imag * focus_imag
    part_imag = square_real * focus_imag + square_imag * focus_real
    partial_image = jnp.stack([part_real, part_imag])
    return all_sum_once(partial_image, "freq", freqs)


def solution(mesh):
    in_specs = (
        P("tile", None, "freq"),
        P("tile", None),
        P("freq"),
        P("freq", None, None),
        P("freq", None, "tile", None),
    )
    out_specs = P(None, "tile", None)
    return jax.shard_map(body, mesh=mesh, in_specs=in_specs, out_specs=out_specs, check_vma=False)
```

```python
import math

import jax
import jax.numpy as jnp
from jax import lax
from jax.sharding import PartitionSpec as P

TWO_PI = 2.0 * math.pi


def gather_shifted(block, axis_name, size):
    pieces = [block]
    for s in range(1, size):
        pairs = [(i, (i - s) % size) for i in range(size)]
        pieces.append(lax.ppermute(block, axis_name, pairs))
    return pieces


def chain(block, axis_name, size, stride, step, direction):
    positions = size // stride
    pairs = []
    for z in range(positions):
        target = z + direction
        if 0 <= target < positions and 0 <= z - direction * (step - 1) < positions:
            pairs += [(z * stride + y, target * stride + y) for y in range(stride)]
    return lax.ppermute(block, axis_name, pairs)


def line_gather(block, axis_name, size):
    positions = size // 2
    z = lax.axis_index(axis_name) // 2
    left = [block]
    right = [block]
    for j in range(1, positions):
        left.append(chain(left[-1], axis_name, size, 2, j, 1))
        right.append(chain(right[-1], axis_name, size, 2, j, -1))
    slots = left[:0:-1] + [block] + right[1:]
    return slots, z


def pair_swap(slots, axis_name, size):
    positions = size // 2
    centre = positions - 1
    out = []
    for i, piece in enumerate(slots):
        d = i - centre
        pairs = [(p * 2 + y, p * 2 + 1 - y) for p in range(positions) if 0 <= p + d < positions for y in range(2)]
        out.append(lax.ppermute(piece, axis_name, pairs))
    return out


def gather_rows(block, axis_name, size):
    positions = size // 2
    slots, z = line_gather(block, axis_name, size)
    other = pair_swap(slots, axis_name, size)
    mine = lax.dynamic_slice_in_dim(jnp.stack(slots), positions - 1 - z, positions, 0)
    theirs = lax.dynamic_slice_in_dim(jnp.stack(other), positions - 1 - z, positions, 0)
    both = jnp.stack([mine, theirs], axis=1)
    both = jnp.roll(both, lax.axis_index(axis_name) % 2, axis=1)
    return both.reshape((size,) + block.shape)


def gather_columns(block, axis_name, size):
    outer = size // 2
    same_core = [block]
    for s in range(1, outer):
        pairs = [(i, (i - 2 * s) % size) for i in range(size)]
        same_core.append(lax.ppermute(block, axis_name, pairs))
    swap = [(i, i ^ 1) for i in range(size)]
    partner = [lax.ppermute(piece, axis_name, swap) for piece in same_core]
    return jnp.stack([jnp.stack(same_core), jnp.stack(partner)], axis=1)


def gather_row_blocks(block, axis_name, size):
    positions = size // 2
    i = lax.axis_index(axis_name)
    z = i // 2
    y = i % 2
    row = [block]
    for s in range(1, positions):
        pairs = [(p * 2 + r, ((p - s) % positions) * 2 + r) for p in range(positions) for r in range(2)]
        row.append(lax.ppermute(block, axis_name, pairs))
    other = lax.ppermute(jnp.stack(row), axis_name, [(j, j ^ 1) for j in range(size)])
    out = []
    for s in range(positions):
        out.append((((z + s) % positions) * 2 + y, row[s]))
        out.append((((z + s) % positions) * 2 + 1 - y, other[s]))
    return out


def all_sum_once(value, axis_name, size):
    pieces = gather_shifted(value, axis_name, size)
    stacked = jnp.roll(jnp.stack(pieces), lax.axis_index(axis_name), axis=0)
    total = stacked[0]
    for j in range(1, size):
        total = total + stacked[j]
    return total


def all_sum(value, axis_name, size):
    step = 1
    while step < size:
        pairs = [(i, i ^ step) for i in range(size)]
        value = value + lax.ppermute(value, axis_name, pairs)
        step *= 2
    return value


def body(travel_time, crossing, bins, transmission, capture):
    tiles = lax.axis_size("tile")
    freqs = lax.axis_size("freq")
    k = lax.axis_index("tile")
    f = lax.axis_index("freq")

    positions = tiles // 2
    z = k // 2
    y = k % 2
    swap = [(j, j ^ 1) for j in range(tiles)]

    cap_row = [capture[0]]
    for s in range(1, positions):
        pairs = [(p * 2 + r, ((p - s) % positions) * 2 + r) for p in range(positions) for r in range(2)]
        cap_row.append(lax.ppermute(capture[0], "tile", pairs))
    own_swapped = lax.ppermute(capture[0], "tile", swap)

    per_tile = travel_time.shape[1] // tiles
    pieces = [lax.dynamic_slice_in_dim(travel_time, 2 * z * per_tile, 2 * per_tile, 1)]
    for s in range(1, positions):
        target = (z - s) % positions
        sent = lax.dynamic_slice_in_dim(travel_time, 2 * target * per_tile, 2 * per_tile, 1)
        pairs = [(p * 2 + r, ((p - s) % positions) * 2 + r) for p in range(positions) for r in range(2)]
        pieces.append(lax.ppermute(sent, "tile", pairs))
    pieces = jnp.stack(pieces)
    mine_tt = lax.dynamic_slice_in_dim(pieces, y * per_tile, per_tile, 2)
    theirs_tt = lax.ppermute(
        lax.dynamic_slice_in_dim(pieces, (1 - y) * per_tile, per_tile, 2), "tile", [(j, j ^ 1) for j in range(tiles)]
    )
    both_tt = jnp.stack([mine_tt, theirs_tt], axis=1)
    both_tt = jnp.roll(jnp.roll(both_tt, z, axis=0), y, axis=1)
    regrouped = both_tt.reshape((-1,) + both_tt.shape[3:])
    view = gather_columns(regrouped, "freq", freqs)
    view = jnp.moveaxis(view.reshape((freqs,) + regrouped.shape), 0, 2)
    elements, row_count, _, width = view.shape
    voxels = row_count * freqs * width

    turns = bins[0].astype(jnp.float32) * view.reshape(elements, voxels)
    turns = turns - jnp.round(turns)
    quarter = jnp.round(4.0 * turns)
    theta = TWO_PI * (turns - 0.25 * quarter)
    theta2 = theta * theta
    sine = theta * (1.0 + theta2 * (-1.0 / 6.0 + theta2 * (1.0 / 120.0 + theta2 * (-1.0 / 5040.0 + theta2 / 362880.0))))
    cosine = 1.0 + theta2 * (-0.5 + theta2 * (1.0 / 24.0 + theta2 * (-1.0 / 720.0 + theta2 * (1.0 / 40320.0))))
    q = quarter.astype(jnp.int32) % 4
    cos_full = jnp.where(q == 0, cosine, jnp.where(q == 1, -sine, jnp.where(q == 2, -cosine, sine)))
    sin_full = jnp.where(q == 0, sine, jnp.where(q == 1, cosine, jnp.where(q == 2, -sine, -cosine)))
    field_real = cos_full.astype(jnp.bfloat16)
    field_imag = (-sin_full).astype(jnp.bfloat16)
    left = jnp.concatenate([field_real, field_imag], axis=1)
    right = jnp.concatenate([-field_imag, field_real], axis=1)

    row = cap_row
    other = (own_swapped, lax.ppermute(jnp.stack(row[1:]), "tile", swap))
    row = jnp.stack(row)
    own = capture.shape[2]

    def rows_of(field, which_row):
        grid = field.reshape(positions, 2, own, voxels)
        picked = lax.dynamic_index_in_dim(grid, which_row, 1, keepdims=False)
        return jnp.roll(picked, -z, axis=0).reshape(-1, voxels)

    def partial_focus(group, g_real, g_imag):
        cap_real = group[:, 0].reshape(-1, group.shape[-1])
        cap_imag = group[:, 1].reshape(-1, group.shape[-1])
        product = jnp.dot(cap_real, left, preferred_element_type=jnp.float32) + jnp.dot(
            cap_imag, right, preferred_element_type=jnp.float32
        )
        w_real = product[:, :voxels]
        w_imag = product[:, voxels:]
        g_real = g_real.astype(jnp.float32)
        g_imag = g_imag.astype(jnp.float32)
        part_real = jnp.sum(g_real * w_real - g_imag * w_imag, axis=0)
        part_imag = jnp.sum(g_real * w_imag + g_imag * w_real, axis=0)
        return part_real, part_imag

    mine_real, mine_imag = partial_focus(row, rows_of(field_real, y), rows_of(field_imag, y))
    theirs_rows = (rows_of(field_real, 1 - y), rows_of(field_imag, 1 - y))
    mine_real, mine_imag, theirs_rows, other = lax.optimization_barrier((mine_real, mine_imag, theirs_rows, other))
    theirs_real, theirs_imag = partial_focus(jnp.concatenate([other[0][None], other[1]]), *theirs_rows)
    focus_real = mine_real + theirs_real
    focus_imag = mine_imag + theirs_imag

    outer = freqs // 2
    focus = jnp.stack([focus_real, focus_imag]).reshape(2, row_count, outer, 2, width)
    focus = jnp.roll(focus, f % 2, axis=3)
    focus = jnp.roll(focus, f // 2, axis=2).reshape(2, row_count, freqs * width)
    focus_real = focus[0]
    focus_imag = focus[1]

    cells = transmission.shape[2]
    match = crossing[None] == lax.broadcasted_iota(jnp.int32, (cells, 1, 1), 0)
    coeff_real = jnp.sum(jnp.where(match, transmission[0, 0][:, None, None], jnp.float32(0.0)), axis=0)
    coeff_imag = jnp.sum(jnp.where(match, transmission[0, 1][:, None, None], jnp.float32(0.0)), axis=0)
    square_real = coeff_real * coeff_real - coeff_imag * coeff_imag
    square_imag = 2.0 * coeff_real * coeff_imag
    part_real = square_real * focus_real - square_imag * focus_imag
    part_imag = square_real * focus_imag + square_imag * focus_real
    partial_image = jnp.stack([part_real, part_imag])
    return all_sum_once(partial_image, "freq", freqs)


def solution(mesh):
    in_specs = (
        P("tile", None, "freq"),
        P("tile", None),
        P("freq"),
        P("freq", None, None),
        P("freq", None, "tile", None),
    )
    out_specs = P(None, "tile", None)
    return jax.shard_map(body, mesh=mesh, in_specs=in_specs, out_specs=out_specs, check_vma=False)
```

```python
import math

import jax
import jax.numpy as jnp
from jax import lax
from jax.sharding import PartitionSpec as P

TWO_PI = 2.0 * math.pi


def gather_shifted(block, axis_name, size):
    pieces = [block]
    for s in range(1, size):
        pairs = [(i, (i - s) % size) for i in range(size)]
        pieces.append(lax.ppermute(block, axis_name, pairs))
    return pieces


def chain(block, axis_name, size, stride, step, direction):
    positions = size // stride
    pairs = []
    for z in range(positions):
        target = z + direction
        if 0 <= target < positions and 0 <= z - direction * (step - 1) < positions:
            pairs += [(z * stride + y, target * stride + y) for y in range(stride)]
    return lax.ppermute(block, axis_name, pairs)


def line_gather(block, axis_name, size):
    positions = size // 2
    z = lax.axis_index(axis_name) // 2
    left = [block]
    right = [block]
    for j in range(1, positions):
        left.append(chain(left[-1], axis_name, size, 2, j, 1))
        right.append(chain(right[-1], axis_name, size, 2, j, -1))
    slots = left[:0:-1] + [block] + right[1:]
    return slots, z


def pair_swap(slots, axis_name, size):
    positions = size // 2
    centre = positions - 1
    out = []
    for i, piece in enumerate(slots):
        d = i - centre
        pairs = [(p * 2 + y, p * 2 + 1 - y) for p in range(positions) if 0 <= p + d < positions for y in range(2)]
        out.append(lax.ppermute(piece, axis_name, pairs))
    return out


def gather_rows(block, axis_name, size):
    positions = size // 2
    slots, z = line_gather(block, axis_name, size)
    other = pair_swap(slots, axis_name, size)
    mine = lax.dynamic_slice_in_dim(jnp.stack(slots), positions - 1 - z, positions, 0)
    theirs = lax.dynamic_slice_in_dim(jnp.stack(other), positions - 1 - z, positions, 0)
    both = jnp.stack([mine, theirs], axis=1)
    both = jnp.roll(both, lax.axis_index(axis_name) % 2, axis=1)
    return both.reshape((size,) + block.shape)


def gather_columns(block, axis_name, size):
    outer = size // 2
    same_core = [block]
    for s in range(1, outer):
        pairs = [(i, (i - 2 * s) % size) for i in range(size)]
        same_core.append(lax.ppermute(block, axis_name, pairs))
    swap = [(i, i ^ 1) for i in range(size)]
    partner = [lax.ppermute(piece, axis_name, swap) for piece in same_core]
    return jnp.stack([jnp.stack(same_core), jnp.stack(partner)], axis=1)


def gather_row_blocks(block, axis_name, size):
    positions = size // 2
    i = lax.axis_index(axis_name)
    z = i // 2
    y = i % 2
    row = [block]
    for s in range(1, positions):
        pairs = [(p * 2 + r, ((p - s) % positions) * 2 + r) for p in range(positions) for r in range(2)]
        row.append(lax.ppermute(block, axis_name, pairs))
    other = lax.ppermute(jnp.stack(row), axis_name, [(j, j ^ 1) for j in range(size)])
    out = []
    for s in range(positions):
        out.append((((z + s) % positions) * 2 + y, row[s]))
        out.append((((z + s) % positions) * 2 + 1 - y, other[s]))
    return out


def all_sum_once(value, axis_name, size):
    pieces = gather_shifted(value, axis_name, size)
    stacked = jnp.roll(jnp.stack(pieces), lax.axis_index(axis_name), axis=0)
    total = stacked[0]
    for j in range(1, size):
        total = total + stacked[j]
    return total


def all_sum(value, axis_name, size):
    step = 1
    while step < size:
        pairs = [(i, i ^ step) for i in range(size)]
        value = value + lax.ppermute(value, axis_name, pairs)
        step *= 2
    return value


def body(travel_time, crossing, bins, transmission, capture):
    tiles = lax.axis_size("tile")
    freqs = lax.axis_size("freq")
    k = lax.axis_index("tile")
    f = lax.axis_index("freq")

    positions = tiles // 2
    z = k // 2
    y = k % 2
    swap = [(j, j ^ 1) for j in range(tiles)]

    cap_row = [capture[0]]
    for s in range(1, positions):
        pairs = [(p * 2 + r, ((p - s) % positions) * 2 + r) for p in range(positions) for r in range(2)]
        cap_row.append(lax.ppermute(capture[0], "tile", pairs))
    own_swapped = lax.ppermute(capture[0], "tile", swap)

    per_tile = travel_time.shape[1] // tiles
    pieces = [lax.dynamic_slice_in_dim(travel_time, 2 * z * per_tile, 2 * per_tile, 1)]
    for s in range(1, positions):
        target = (z - s) % positions
        sent = lax.dynamic_slice_in_dim(travel_time, 2 * target * per_tile, 2 * per_tile, 1)
        pairs = [(p * 2 + r, ((p - s) % positions) * 2 + r) for p in range(positions) for r in range(2)]
        pieces.append(lax.ppermute(sent, "tile", pairs))
    pieces = jnp.stack(pieces)
    mine_tt = lax.dynamic_slice_in_dim(pieces, y * per_tile, per_tile, 2)
    theirs_tt = lax.ppermute(
        lax.dynamic_slice_in_dim(pieces, (1 - y) * per_tile, per_tile, 2), "tile", [(j, j ^ 1) for j in range(tiles)]
    )
    both_tt = jnp.stack([mine_tt, theirs_tt], axis=1)
    both_tt = jnp.roll(jnp.roll(both_tt, z, axis=0), y, axis=1)
    regrouped = both_tt.reshape((-1,) + both_tt.shape[3:])
    view = gather_columns(regrouped, "freq", freqs)
    view = jnp.moveaxis(view.reshape((freqs,) + regrouped.shape), 0, 2)
    elements, row_count, _, width = view.shape
    voxels = row_count * freqs * width

    scaled = TWO_PI * bins[0].astype(jnp.float32)
    angle = scaled * view.reshape(elements, voxels)
    field_real = jnp.cos(angle).astype(jnp.bfloat16)
    field_imag = (-jnp.sin(angle)).astype(jnp.bfloat16)

    row = cap_row
    other = (own_swapped, lax.ppermute(jnp.stack(row[1:]), "tile", swap))
    row = jnp.stack(row)
    own = capture.shape[2]

    def rows_of(field, which_row):
        grid = field.reshape(positions, 2, own, voxels)
        picked = lax.dynamic_index_in_dim(grid, which_row, 1, keepdims=False)
        return jnp.roll(picked, -z, axis=0).reshape(-1, voxels)

    def partial_focus(group, g_real, g_imag):
        cap_real = group[:, 0].reshape(-1, group.shape[-1])
        cap_imag = group[:, 1].reshape(-1, group.shape[-1])
        w_real = jnp.dot(cap_real, field_real, preferred_element_type=jnp.float32) - jnp.dot(
            cap_imag, field_imag, preferred_element_type=jnp.float32
        )
        w_imag = jnp.dot(cap_real, field_imag, preferred_element_type=jnp.float32) + jnp.dot(
            cap_imag, field_real, preferred_element_type=jnp.float32
        )
        g_real = g_real.astype(jnp.float32)
        g_imag = g_imag.astype(jnp.float32)
        part_real = jnp.sum(g_real * w_real - g_imag * w_imag, axis=0)
        part_imag = jnp.sum(g_real * w_imag + g_imag * w_real, axis=0)
        return part_real, part_imag

    mine_real, mine_imag = partial_focus(row, rows_of(field_real, y), rows_of(field_imag, y))
    theirs_rows = (rows_of(field_real, 1 - y), rows_of(field_imag, 1 - y))
    mine_real, mine_imag, theirs_rows, other = lax.optimization_barrier((mine_real, mine_imag, theirs_rows, other))
    theirs_real, theirs_imag = partial_focus(jnp.concatenate([other[0][None], other[1]]), *theirs_rows)
    focus_real = mine_real + theirs_real
    focus_imag = mine_imag + theirs_imag

    outer = freqs // 2
    focus = jnp.stack([focus_real, focus_imag]).reshape(2, row_count, outer, 2, width)
    focus = jnp.roll(focus, f % 2, axis=3)
    focus = jnp.roll(focus, f // 2, axis=2).reshape(2, row_count, freqs * width)
    focus_real = focus[0]
    focus_imag = focus[1]

    cells = transmission.shape[2]
    match = crossing[None] == lax.broadcasted_iota(jnp.int32, (cells, 1, 1), 0)
    coeff_real = jnp.sum(jnp.where(match, transmission[0, 0][:, None, None], jnp.float32(0.0)), axis=0)
    coeff_imag = jnp.sum(jnp.where(match, transmission[0, 1][:, None, None], jnp.float32(0.0)), axis=0)
    square_real = coeff_real * coeff_real - coeff_imag * coeff_imag
    square_imag = 2.0 * coeff_real * coeff_imag
    part_real = square_real * focus_real - square_imag * focus_imag
    part_imag = square_real * focus_imag + square_imag * focus_real
    partial_image = jnp.stack([part_real, part_imag])
    return all_sum_once(partial_image, "freq", freqs)


def solution(mesh):
    in_specs = (
        P("tile", None, "freq"),
        P("tile", None),
        P("freq"),
        P("freq", None, None),
        P("freq", None, "tile", None),
    )
    out_specs = P(None, "tile", None)
    return jax.shard_map(body, mesh=mesh, in_specs=in_specs, out_specs=out_specs, check_vma=False)
```

```python
import math

import jax
import jax.numpy as jnp
from jax import lax
from jax.sharding import PartitionSpec as P

TWO_PI = 2.0 * math.pi


def gather_shifted(block, axis_name, size):
    pieces = [block]
    for s in range(1, size):
        pairs = [(i, (i - s) % size) for i in range(size)]
        pieces.append(lax.ppermute(block, axis_name, pairs))
    return pieces


def chain(block, axis_name, size, stride, step, direction):
    positions = size // stride
    pairs = []
    for z in range(positions):
        target = z + direction
        if 0 <= target < positions and 0 <= z - direction * (step - 1) < positions:
            pairs += [(z * stride + y, target * stride + y) for y in range(stride)]
    return lax.ppermute(block, axis_name, pairs)


def line_gather(block, axis_name, size):
    positions = size // 2
    z = lax.axis_index(axis_name) // 2
    left = [block]
    right = [block]
    for j in range(1, positions):
        left.append(chain(left[-1], axis_name, size, 2, j, 1))
        right.append(chain(right[-1], axis_name, size, 2, j, -1))
    slots = left[:0:-1] + [block] + right[1:]
    return slots, z


def pair_swap(slots, axis_name, size):
    positions = size // 2
    centre = positions - 1
    out = []
    for i, piece in enumerate(slots):
        d = i - centre
        pairs = [(p * 2 + y, p * 2 + 1 - y) for p in range(positions) if 0 <= p + d < positions for y in range(2)]
        out.append(lax.ppermute(piece, axis_name, pairs))
    return out


def gather_rows(block, axis_name, size):
    positions = size // 2
    slots, z = line_gather(block, axis_name, size)
    other = pair_swap(slots, axis_name, size)
    mine = lax.dynamic_slice_in_dim(jnp.stack(slots), positions - 1 - z, positions, 0)
    theirs = lax.dynamic_slice_in_dim(jnp.stack(other), positions - 1 - z, positions, 0)
    both = jnp.stack([mine, theirs], axis=1)
    both = jnp.roll(both, lax.axis_index(axis_name) % 2, axis=1)
    return both.reshape((size,) + block.shape)


def gather_columns(block, axis_name, size):
    outer = size // 2
    same_core = [block]
    for s in range(1, outer):
        pairs = [(i, (i - 2 * s) % size) for i in range(size)]
        same_core.append(lax.ppermute(block, axis_name, pairs))
    swap = [(i, i ^ 1) for i in range(size)]
    partner = [lax.ppermute(piece, axis_name, swap) for piece in same_core]
    return jnp.stack([jnp.stack(same_core), jnp.stack(partner)], axis=1)


def gather_row_blocks(block, axis_name, size):
    positions = size // 2
    i = lax.axis_index(axis_name)
    z = i // 2
    y = i % 2
    row = [block]
    for s in range(1, positions):
        pairs = [(p * 2 + r, ((p - s) % positions) * 2 + r) for p in range(positions) for r in range(2)]
        row.append(lax.ppermute(block, axis_name, pairs))
    other = lax.ppermute(jnp.stack(row), axis_name, [(j, j ^ 1) for j in range(size)])
    out = []
    for s in range(positions):
        out.append((((z + s) % positions) * 2 + y, row[s]))
        out.append((((z + s) % positions) * 2 + 1 - y, other[s]))
    return out


def all_sum_once(value, axis_name, size):
    pieces = gather_shifted(value, axis_name, size)
    stacked = jnp.roll(jnp.stack(pieces), lax.axis_index(axis_name), axis=0)
    total = stacked[0]
    for j in range(1, size):
        total = total + stacked[j]
    return total


def all_sum(value, axis_name, size):
    step = 1
    while step < size:
        pairs = [(i, i ^ step) for i in range(size)]
        value = value + lax.ppermute(value, axis_name, pairs)
        step *= 2
    return value


def body(travel_time, crossing, bins, transmission, capture):
    tiles = lax.axis_size("tile")
    freqs = lax.axis_size("freq")
    k = lax.axis_index("tile")
    f = lax.axis_index("freq")

    positions = tiles // 2
    z = k // 2
    y = k % 2
    swap = [(j, j ^ 1) for j in range(tiles)]

    cap_row = [capture[0]]
    for s in range(1, positions):
        pairs = [(p * 2 + r, ((p - s) % positions) * 2 + r) for p in range(positions) for r in range(2)]
        cap_row.append(lax.ppermute(capture[0], "tile", pairs))
    own_swapped = lax.ppermute(capture[0], "tile", swap)

    per_tile = travel_time.shape[1] // tiles
    by_row = jnp.transpose(travel_time, (1, 0, 2))
    pieces = [lax.dynamic_slice_in_dim(by_row, 2 * z * per_tile, 2 * per_tile, 0)]
    for s in range(1, positions):
        target = (z - s) % positions
        sent = lax.dynamic_slice_in_dim(by_row, 2 * target * per_tile, 2 * per_tile, 0)
        pairs = [(p * 2 + r, ((p - s) % positions) * 2 + r) for p in range(positions) for r in range(2)]
        pieces.append(lax.ppermute(sent, "tile", pairs))
    pieces = jnp.moveaxis(jnp.stack(pieces), 2, 1)
    mine_tt = lax.dynamic_slice_in_dim(pieces, y * per_tile, per_tile, 2)
    theirs_tt = lax.ppermute(
        lax.dynamic_slice_in_dim(pieces, (1 - y) * per_tile, per_tile, 2), "tile", [(j, j ^ 1) for j in range(tiles)]
    )
    both_tt = jnp.stack([mine_tt, theirs_tt], axis=1)
    both_tt = jnp.roll(jnp.roll(both_tt, z, axis=0), y, axis=1)
    regrouped = both_tt.reshape((-1,) + both_tt.shape[3:])
    view = gather_columns(regrouped, "freq", freqs)
    view = jnp.moveaxis(view.reshape((freqs,) + regrouped.shape), 0, 2)
    elements, row_count, _, width = view.shape
    voxels = row_count * freqs * width

    scaled = TWO_PI * bins[0].astype(jnp.float32)
    angle = scaled * view.reshape(elements, voxels)
    field_real = jnp.cos(angle).astype(jnp.bfloat16)
    field_imag = (-jnp.sin(angle)).astype(jnp.bfloat16)
    left = jnp.concatenate([field_real, field_imag], axis=1)
    right = jnp.concatenate([-field_imag, field_real], axis=1)

    row = cap_row
    other = (own_swapped, lax.ppermute(jnp.stack(row[1:]), "tile", swap))
    row = jnp.stack(row)
    own = capture.shape[2]

    def rows_of(field, which_row):
        grid = field.reshape(positions, 2, own, voxels)
        picked = lax.dynamic_index_in_dim(grid, which_row, 1, keepdims=False)
        return jnp.roll(picked, -z, axis=0).reshape(-1, voxels)

    def partial_focus(group, g_real, g_imag):
        cap_real = group[:, 0].reshape(-1, group.shape[-1])
        cap_imag = group[:, 1].reshape(-1, group.shape[-1])
        product = jnp.dot(cap_real, left, preferred_element_type=jnp.float32) + jnp.dot(
            cap_imag, right, preferred_element_type=jnp.float32
        )
        w_real = product[:, :voxels]
        w_imag = product[:, voxels:]
        g_real = g_real.astype(jnp.float32)
        g_imag = g_imag.astype(jnp.float32)
        part_real = jnp.sum(g_real * w_real - g_imag * w_imag, axis=0)
        part_imag = jnp.sum(g_real * w_imag + g_imag * w_real, axis=0)
        return part_real, part_imag

    mine_real, mine_imag = partial_focus(row, rows_of(field_real, y), rows_of(field_imag, y))
    theirs_rows = (rows_of(field_real, 1 - y), rows_of(field_imag, 1 - y))
    mine_real, mine_imag, theirs_rows, other = lax.optimization_barrier((mine_real, mine_imag, theirs_rows, other))
    theirs_real, theirs_imag = partial_focus(jnp.concatenate([other[0][None], other[1]]), *theirs_rows)
    focus_real = mine_real + theirs_real
    focus_imag = mine_imag + theirs_imag

    outer = freqs // 2
    focus = jnp.stack([focus_real, focus_imag]).reshape(2, row_count, outer, 2, width)
    focus = jnp.roll(focus, f % 2, axis=3)
    focus = jnp.roll(focus, f // 2, axis=2).reshape(2, row_count, freqs * width)
    focus_real = focus[0]
    focus_imag = focus[1]

    cells = transmission.shape[2]
    match = crossing[None] == lax.broadcasted_iota(jnp.int32, (cells, 1, 1), 0)
    coeff_real = jnp.sum(jnp.where(match, transmission[0, 0][:, None, None], jnp.float32(0.0)), axis=0)
    coeff_imag = jnp.sum(jnp.where(match, transmission[0, 1][:, None, None], jnp.float32(0.0)), axis=0)
    square_real = coeff_real * coeff_real - coeff_imag * coeff_imag
    square_imag = 2.0 * coeff_real * coeff_imag
    part_real = square_real * focus_real - square_imag * focus_imag
    part_imag = square_real * focus_imag + square_imag * focus_real
    partial_image = jnp.stack([part_real, part_imag])
    return all_sum_once(partial_image, "freq", freqs)


def solution(mesh):
    in_specs = (
        P("tile", None, "freq"),
        P("tile", None),
        P("freq"),
        P("freq", None, None),
        P("freq", None, "tile", None),
    )
    out_specs = P(None, "tile", None)
    return jax.shard_map(body, mesh=mesh, in_specs=in_specs, out_specs=out_specs, check_vma=False)
```

```python
import math

import jax
import jax.numpy as jnp
from jax import lax
from jax.sharding import PartitionSpec as P

TWO_PI = 2.0 * math.pi


def gather_shifted(block, axis_name, size):
    pieces = [block]
    for s in range(1, size):
        pairs = [(i, (i - s) % size) for i in range(size)]
        pieces.append(lax.ppermute(block, axis_name, pairs))
    return pieces


def chain(block, axis_name, size, stride, step, direction):
    positions = size // stride
    pairs = []
    for z in range(positions):
        target = z + direction
        if 0 <= target < positions and 0 <= z - direction * (step - 1) < positions:
            pairs += [(z * stride + y, target * stride + y) for y in range(stride)]
    return lax.ppermute(block, axis_name, pairs)


def line_gather(block, axis_name, size):
    positions = size // 2
    z = lax.axis_index(axis_name) // 2
    left = [block]
    right = [block]
    for j in range(1, positions):
        left.append(chain(left[-1], axis_name, size, 2, j, 1))
        right.append(chain(right[-1], axis_name, size, 2, j, -1))
    slots = left[:0:-1] + [block] + right[1:]
    return slots, z


def pair_swap(slots, axis_name, size):
    positions = size // 2
    centre = positions - 1
    out = []
    for i, piece in enumerate(slots):
        d = i - centre
        pairs = [(p * 2 + y, p * 2 + 1 - y) for p in range(positions) if 0 <= p + d < positions for y in range(2)]
        out.append(lax.ppermute(piece, axis_name, pairs))
    return out


def gather_rows(block, axis_name, size):
    positions = size // 2
    slots, z = line_gather(block, axis_name, size)
    other = pair_swap(slots, axis_name, size)
    mine = lax.dynamic_slice_in_dim(jnp.stack(slots), positions - 1 - z, positions, 0)
    theirs = lax.dynamic_slice_in_dim(jnp.stack(other), positions - 1 - z, positions, 0)
    both = jnp.stack([mine, theirs], axis=1)
    both = jnp.roll(both, lax.axis_index(axis_name) % 2, axis=1)
    return both.reshape((size,) + block.shape)


def gather_columns(block, axis_name, size):
    outer = size // 2
    same_core = [block]
    for s in range(1, outer):
        pairs = [(i, (i - 2 * s) % size) for i in range(size)]
        same_core.append(lax.ppermute(block, axis_name, pairs))
    swap = [(i, i ^ 1) for i in range(size)]
    partner = [lax.ppermute(piece, axis_name, swap) for piece in same_core]
    return jnp.stack([jnp.stack(same_core), jnp.stack(partner)], axis=1)


def gather_row_blocks(block, axis_name, size):
    positions = size // 2
    i = lax.axis_index(axis_name)
    z = i // 2
    y = i % 2
    row = [block]
    for s in range(1, positions):
        pairs = [(p * 2 + r, ((p - s) % positions) * 2 + r) for p in range(positions) for r in range(2)]
        row.append(lax.ppermute(block, axis_name, pairs))
    other = lax.ppermute(jnp.stack(row), axis_name, [(j, j ^ 1) for j in range(size)])
    out = []
    for s in range(positions):
        out.append((((z + s) % positions) * 2 + y, row[s]))
        out.append((((z + s) % positions) * 2 + 1 - y, other[s]))
    return out


def all_sum_once(value, axis_name, size):
    pieces = gather_shifted(value, axis_name, size)
    stacked = jnp.roll(jnp.stack(pieces), lax.axis_index(axis_name), axis=0)
    total = stacked[0]
    for j in range(1, size):
        total = total + stacked[j]
    return total


def all_sum(value, axis_name, size):
    step = 1
    while step < size:
        pairs = [(i, i ^ step) for i in range(size)]
        value = value + lax.ppermute(value, axis_name, pairs)
        step *= 2
    return value


def body(travel_time, crossing, bins, transmission, capture):
    tiles = lax.axis_size("tile")
    freqs = lax.axis_size("freq")
    k = lax.axis_index("tile")
    f = lax.axis_index("freq")

    positions = tiles // 2
    z = k // 2
    y = k % 2
    swap = [(j, j ^ 1) for j in range(tiles)]

    cap_row = [capture[0]]
    for s in range(1, positions):
        pairs = [(p * 2 + r, ((p - s) % positions) * 2 + r) for p in range(positions) for r in range(2)]
        cap_row.append(lax.ppermute(capture[0], "tile", pairs))

    per_tile = travel_time.shape[1] // tiles
    pieces = [lax.dynamic_slice_in_dim(travel_time, 2 * z * per_tile, 2 * per_tile, 1)]
    for s in range(1, positions):
        target = (z - s) % positions
        sent = lax.dynamic_slice_in_dim(travel_time, 2 * target * per_tile, 2 * per_tile, 1)
        pairs = [(p * 2 + r, ((p - s) % positions) * 2 + r) for p in range(positions) for r in range(2)]
        pieces.append(lax.ppermute(sent, "tile", pairs))
    pieces = jnp.stack(pieces)
    mine_tt = lax.dynamic_slice_in_dim(pieces, y * per_tile, per_tile, 2)
    theirs_tt = lax.ppermute(
        lax.dynamic_slice_in_dim(pieces, (1 - y) * per_tile, per_tile, 2), "tile", [(j, j ^ 1) for j in range(tiles)]
    )
    cap_own, theirs_tt = lax.optimization_barrier((capture[0], theirs_tt))
    own_swapped = lax.ppermute(cap_own, "tile", swap)
    both_tt = jnp.stack([mine_tt, theirs_tt], axis=1)
    both_tt = jnp.roll(jnp.roll(both_tt, z, axis=0), y, axis=1)
    regrouped = both_tt.reshape((-1,) + both_tt.shape[3:])
    view = gather_columns(regrouped, "freq", freqs)
    view = jnp.moveaxis(view.reshape((freqs,) + regrouped.shape), 0, 2)
    elements, row_count, _, width = view.shape
    voxels = row_count * freqs * width

    scaled = TWO_PI * bins[0].astype(jnp.float32)
    angle = scaled * view.reshape(elements, voxels)
    field_real = jnp.cos(angle).astype(jnp.bfloat16)
    field_imag = (-jnp.sin(angle)).astype(jnp.bfloat16)
    left = jnp.concatenate([field_real, field_imag], axis=1)
    right = jnp.concatenate([-field_imag, field_real], axis=1)

    row = cap_row
    other = (own_swapped, lax.ppermute(jnp.stack(row[1:]), "tile", swap))
    row = jnp.stack(row)
    own = capture.shape[2]

    def rows_of(field, which_row):
        grid = field.reshape(positions, 2, own, voxels)
        picked = lax.dynamic_index_in_dim(grid, which_row, 1, keepdims=False)
        return jnp.roll(picked, -z, axis=0).reshape(-1, voxels)

    def partial_focus(group, g_real, g_imag):
        cap_real = group[:, 0].reshape(-1, group.shape[-1])
        cap_imag = group[:, 1].reshape(-1, group.shape[-1])
        product = jnp.dot(cap_real, left, preferred_element_type=jnp.float32) + jnp.dot(
            cap_imag, right, preferred_element_type=jnp.float32
        )
        w_real = product[:, :voxels]
        w_imag = product[:, voxels:]
        g_real = g_real.astype(jnp.float32)
        g_imag = g_imag.astype(jnp.float32)
        part_real = jnp.sum(g_real * w_real - g_imag * w_imag, axis=0)
        part_imag = jnp.sum(g_real * w_imag + g_imag * w_real, axis=0)
        return part_real, part_imag

    mine_real, mine_imag = partial_focus(row, rows_of(field_real, y), rows_of(field_imag, y))
    theirs_rows = (rows_of(field_real, 1 - y), rows_of(field_imag, 1 - y))
    mine_real, mine_imag, theirs_rows, other = lax.optimization_barrier((mine_real, mine_imag, theirs_rows, other))
    theirs_real, theirs_imag = partial_focus(jnp.concatenate([other[0][None], other[1]]), *theirs_rows)
    focus_real = mine_real + theirs_real
    focus_imag = mine_imag + theirs_imag

    outer = freqs // 2
    focus = jnp.stack([focus_real, focus_imag]).reshape(2, row_count, outer, 2, width)
    focus = jnp.roll(focus, f % 2, axis=3)
    focus = jnp.roll(focus, f // 2, axis=2).reshape(2, row_count, freqs * width)
    focus_real = focus[0]
    focus_imag = focus[1]

    cells = transmission.shape[2]
    match = crossing[None] == lax.broadcasted_iota(jnp.int32, (cells, 1, 1), 0)
    coeff_real = jnp.sum(jnp.where(match, transmission[0, 0][:, None, None], jnp.float32(0.0)), axis=0)
    coeff_imag = jnp.sum(jnp.where(match, transmission[0, 1][:, None, None], jnp.float32(0.0)), axis=0)
    square_real = coeff_real * coeff_real - coeff_imag * coeff_imag
    square_imag = 2.0 * coeff_real * coeff_imag
    part_real = square_real * focus_real - square_imag * focus_imag
    part_imag = square_real * focus_imag + square_imag * focus_real
    partial_image = jnp.stack([part_real, part_imag])
    return all_sum_once(partial_image, "freq", freqs)


def solution(mesh):
    in_specs = (
        P("tile", None, "freq"),
        P("tile", None),
        P("freq"),
        P("freq", None, None),
        P("freq", None, "tile", None),
    )
    out_specs = P(None, "tile", None)
    return jax.shard_map(body, mesh=mesh, in_specs=in_specs, out_specs=out_specs, check_vma=False)
```

```python
import math

import jax
import jax.numpy as jnp
from jax import lax
from jax.sharding import PartitionSpec as P

TWO_PI = 2.0 * math.pi


def gather_shifted(block, axis_name, size):
    pieces = [block]
    for s in range(1, size):
        pairs = [(i, (i - s) % size) for i in range(size)]
        pieces.append(lax.ppermute(block, axis_name, pairs))
    return pieces


def chain(block, axis_name, size, stride, step, direction):
    positions = size // stride
    pairs = []
    for z in range(positions):
        target = z + direction
        if 0 <= target < positions and 0 <= z - direction * (step - 1) < positions:
            pairs += [(z * stride + y, target * stride + y) for y in range(stride)]
    return lax.ppermute(block, axis_name, pairs)


def line_gather(block, axis_name, size):
    positions = size // 2
    z = lax.axis_index(axis_name) // 2
    left = [block]
    right = [block]
    for j in range(1, positions):
        left.append(chain(left[-1], axis_name, size, 2, j, 1))
        right.append(chain(right[-1], axis_name, size, 2, j, -1))
    slots = left[:0:-1] + [block] + right[1:]
    return slots, z


def pair_swap(slots, axis_name, size):
    positions = size // 2
    centre = positions - 1
    out = []
    for i, piece in enumerate(slots):
        d = i - centre
        pairs = [(p * 2 + y, p * 2 + 1 - y) for p in range(positions) if 0 <= p + d < positions for y in range(2)]
        out.append(lax.ppermute(piece, axis_name, pairs))
    return out


def gather_rows(block, axis_name, size):
    positions = size // 2
    slots, z = line_gather(block, axis_name, size)
    other = pair_swap(slots, axis_name, size)
    mine = lax.dynamic_slice_in_dim(jnp.stack(slots), positions - 1 - z, positions, 0)
    theirs = lax.dynamic_slice_in_dim(jnp.stack(other), positions - 1 - z, positions, 0)
    both = jnp.stack([mine, theirs], axis=1)
    both = jnp.roll(both, lax.axis_index(axis_name) % 2, axis=1)
    return both.reshape((size,) + block.shape)


def gather_columns(block, axis_name, size):
    outer = size // 2
    same_core = [block]
    for s in range(1, outer):
        pairs = [(i, (i - 2 * s) % size) for i in range(size)]
        same_core.append(lax.ppermute(block, axis_name, pairs))
    swap = [(i, i ^ 1) for i in range(size)]
    partner = [lax.ppermute(piece, axis_name, swap) for piece in same_core]
    return jnp.stack([jnp.stack(same_core), jnp.stack(partner)], axis=1)


def gather_row_blocks(block, axis_name, size):
    positions = size // 2
    i = lax.axis_index(axis_name)
    z = i // 2
    y = i % 2
    row = [block]
    for s in range(1, positions):
        pairs = [(p * 2 + r, ((p - s) % positions) * 2 + r) for p in range(positions) for r in range(2)]
        row.append(lax.ppermute(block, axis_name, pairs))
    other = lax.ppermute(jnp.stack(row), axis_name, [(j, j ^ 1) for j in range(size)])
    out = []
    for s in range(positions):
        out.append((((z + s) % positions) * 2 + y, row[s]))
        out.append((((z + s) % positions) * 2 + 1 - y, other[s]))
    return out


def all_sum_once(value, axis_name, size):
    pieces = gather_shifted(value, axis_name, size)
    stacked = jnp.roll(jnp.stack(pieces), lax.axis_index(axis_name), axis=0)
    total = stacked[0]
    for j in range(1, size):
        total = total + stacked[j]
    return total


def all_sum(value, axis_name, size):
    step = 1
    while step < size:
        pairs = [(i, i ^ step) for i in range(size)]
        value = value + lax.ppermute(value, axis_name, pairs)
        step *= 2
    return value


def body(travel_time, crossing, bins, transmission, capture):
    tiles = lax.axis_size("tile")
    freqs = lax.axis_size("freq")
    k = lax.axis_index("tile")
    f = lax.axis_index("freq")

    positions = tiles // 2
    z = k // 2
    y = k % 2
    swap = [(j, j ^ 1) for j in range(tiles)]

    cap_row = [capture[0]]
    for s in range(1, positions):
        pairs = [(p * 2 + r, ((p - s) % positions) * 2 + r) for p in range(positions) for r in range(2)]
        cap_row.append(lax.ppermute(capture[0], "tile", pairs))
    own_swapped = lax.ppermute(capture[0], "tile", swap)

    per_tile = travel_time.shape[1] // tiles
    pieces = [lax.dynamic_slice_in_dim(travel_time, 2 * z * per_tile, 2 * per_tile, 1)]
    for s in range(1, positions):
        target = (z - s) % positions
        sent = lax.dynamic_slice_in_dim(travel_time, 2 * target * per_tile, 2 * per_tile, 1)
        pairs = [(p * 2 + r, ((p - s) % positions) * 2 + r) for p in range(positions) for r in range(2)]
        pieces.append(lax.ppermute(sent, "tile", pairs))
    pieces = jnp.stack(pieces)
    mine_tt = lax.dynamic_slice_in_dim(pieces, y * per_tile, per_tile, 2)
    theirs_tt = lax.ppermute(
        lax.dynamic_slice_in_dim(pieces, (1 - y) * per_tile, per_tile, 2), "tile", [(j, j ^ 1) for j in range(tiles)]
    )

    def regroup(mine_part, their_part):
        both = jnp.stack([mine_part, their_part], axis=1)
        both = jnp.roll(jnp.roll(both, z, axis=0), y, axis=1)
        return both.reshape((-1,) + both.shape[3:])

    blocks = [regroup(mine_tt, theirs_tt)]
    for so in range(1, freqs // 2):
        straight = [(i, (i - 2 * so) % freqs) for i in range(freqs)]
        blocks.append(
            regroup(lax.ppermute(mine_tt, "freq", straight), lax.ppermute(theirs_tt, "freq", straight))
        )
    core_swap = [(i, i ^ 1) for i in range(freqs)]
    partner = [lax.ppermute(piece, "freq", core_swap) for piece in blocks]
    regrouped = blocks[0]
    view = jnp.stack([jnp.stack(blocks), jnp.stack(partner)], axis=1)
    view = jnp.moveaxis(view.reshape((freqs,) + regrouped.shape), 0, 2)
    elements, row_count, _, width = view.shape
    voxels = row_count * freqs * width

    scaled = TWO_PI * bins[0].astype(jnp.float32)
    angle = scaled * view.reshape(elements, voxels)
    field_real = jnp.cos(angle).astype(jnp.bfloat16)
    field_imag = (-jnp.sin(angle)).astype(jnp.bfloat16)
    left = jnp.concatenate([field_real, field_imag], axis=1)
    right = jnp.concatenate([-field_imag, field_real], axis=1)

    row = cap_row
    other = (own_swapped, lax.ppermute(jnp.stack(row[1:]), "tile", swap))
    row = jnp.stack(row)
    own = capture.shape[2]

    def rows_of(field, which_row):
        grid = field.reshape(positions, 2, own, voxels)
        picked = lax.dynamic_index_in_dim(grid, which_row, 1, keepdims=False)
        return jnp.roll(picked, -z, axis=0).reshape(-1, voxels)

    def partial_focus(group, g_real, g_imag):
        cap_real = group[:, 0].reshape(-1, group.shape[-1])
        cap_imag = group[:, 1].reshape(-1, group.shape[-1])
        product = jnp.dot(cap_real, left, preferred_element_type=jnp.float32) + jnp.dot(
            cap_imag, right, preferred_element_type=jnp.float32
        )
        w_real = product[:, :voxels]
        w_imag = product[:, voxels:]
        g_real = g_real.astype(jnp.float32)
        g_imag = g_imag.astype(jnp.float32)
        part_real = jnp.sum(g_real * w_real - g_imag * w_imag, axis=0)
        part_imag = jnp.sum(g_real * w_imag + g_imag * w_real, axis=0)
        return part_real, part_imag

    mine_real, mine_imag = partial_focus(row, rows_of(field_real, y), rows_of(field_imag, y))
    theirs_rows = (rows_of(field_real, 1 - y), rows_of(field_imag, 1 - y))
    mine_real, mine_imag, theirs_rows, other = lax.optimization_barrier((mine_real, mine_imag, theirs_rows, other))
    theirs_real, theirs_imag = partial_focus(jnp.concatenate([other[0][None], other[1]]), *theirs_rows)
    focus_real = mine_real + theirs_real
    focus_imag = mine_imag + theirs_imag

    outer = freqs // 2
    focus = jnp.stack([focus_real, focus_imag]).reshape(2, row_count, outer, 2, width)
    focus = jnp.roll(focus, f % 2, axis=3)
    focus = jnp.roll(focus, f // 2, axis=2).reshape(2, row_count, freqs * width)
    focus_real = focus[0]
    focus_imag = focus[1]

    cells = transmission.shape[2]
    match = crossing[None] == lax.broadcasted_iota(jnp.int32, (cells, 1, 1), 0)
    coeff_real = jnp.sum(jnp.where(match, transmission[0, 0][:, None, None], jnp.float32(0.0)), axis=0)
    coeff_imag = jnp.sum(jnp.where(match, transmission[0, 1][:, None, None], jnp.float32(0.0)), axis=0)
    square_real = coeff_real * coeff_real - coeff_imag * coeff_imag
    square_imag = 2.0 * coeff_real * coeff_imag
    part_real = square_real * focus_real - square_imag * focus_imag
    part_imag = square_real * focus_imag + square_imag * focus_real
    partial_image = jnp.stack([part_real, part_imag])
    return all_sum_once(partial_image, "freq", freqs)


def solution(mesh):
    in_specs = (
        P("tile", None, "freq"),
        P("tile", None),
        P("freq"),
        P("freq", None, None),
        P("freq", None, "tile", None),
    )
    out_specs = P(None, "tile", None)
    return jax.shard_map(body, mesh=mesh, in_specs=in_specs, out_specs=out_specs, check_vma=False)
```

```python
import math

import jax
import jax.numpy as jnp
from jax import lax
from jax.sharding import PartitionSpec as P

TWO_PI = 2.0 * math.pi


def gather_shifted(block, axis_name, size):
    pieces = [block]
    for s in range(1, size):
        pairs = [(i, (i - s) % size) for i in range(size)]
        pieces.append(lax.ppermute(block, axis_name, pairs))
    return pieces


def chain(block, axis_name, size, stride, step, direction):
    positions = size // stride
    pairs = []
    for z in range(positions):
        target = z + direction
        if 0 <= target < positions and 0 <= z - direction * (step - 1) < positions:
            pairs += [(z * stride + y, target * stride + y) for y in range(stride)]
    return lax.ppermute(block, axis_name, pairs)


def line_gather(block, axis_name, size):
    positions = size // 2
    z = lax.axis_index(axis_name) // 2
    left = [block]
    right = [block]
    for j in range(1, positions):
        left.append(chain(left[-1], axis_name, size, 2, j, 1))
        right.append(chain(right[-1], axis_name, size, 2, j, -1))
    slots = left[:0:-1] + [block] + right[1:]
    return slots, z


def pair_swap(slots, axis_name, size):
    positions = size // 2
    centre = positions - 1
    out = []
    for i, piece in enumerate(slots):
        d = i - centre
        pairs = [(p * 2 + y, p * 2 + 1 - y) for p in range(positions) if 0 <= p + d < positions for y in range(2)]
        out.append(lax.ppermute(piece, axis_name, pairs))
    return out


def gather_rows(block, axis_name, size):
    positions = size // 2
    slots, z = line_gather(block, axis_name, size)
    other = pair_swap(slots, axis_name, size)
    mine = lax.dynamic_slice_in_dim(jnp.stack(slots), positions - 1 - z, positions, 0)
    theirs = lax.dynamic_slice_in_dim(jnp.stack(other), positions - 1 - z, positions, 0)
    both = jnp.stack([mine, theirs], axis=1)
    both = jnp.roll(both, lax.axis_index(axis_name) % 2, axis=1)
    return both.reshape((size,) + block.shape)


def gather_columns(block, axis_name, size):
    outer = size // 2
    same_core = [block]
    for s in range(1, outer):
        pairs = [(i, (i - 2 * s) % size) for i in range(size)]
        same_core.append(lax.ppermute(block, axis_name, pairs))
    swap = [(i, i ^ 1) for i in range(size)]
    partner = [lax.ppermute(piece, axis_name, swap) for piece in same_core]
    return jnp.stack([jnp.stack(same_core), jnp.stack(partner)], axis=1)


def gather_row_blocks(block, axis_name, size):
    positions = size // 2
    i = lax.axis_index(axis_name)
    z = i // 2
    y = i % 2
    row = [block]
    for s in range(1, positions):
        pairs = [(p * 2 + r, ((p - s) % positions) * 2 + r) for p in range(positions) for r in range(2)]
        row.append(lax.ppermute(block, axis_name, pairs))
    other = lax.ppermute(jnp.stack(row), axis_name, [(j, j ^ 1) for j in range(size)])
    out = []
    for s in range(positions):
        out.append((((z + s) % positions) * 2 + y, row[s]))
        out.append((((z + s) % positions) * 2 + 1 - y, other[s]))
    return out


def all_sum_once(value, axis_name, size):
    pieces = gather_shifted(value, axis_name, size)
    stacked = jnp.roll(jnp.stack(pieces), lax.axis_index(axis_name), axis=0)
    total = stacked[0]
    for j in range(1, size):
        total = total + stacked[j]
    return total


def all_sum(value, axis_name, size):
    step = 1
    while step < size:
        pairs = [(i, i ^ step) for i in range(size)]
        value = value + lax.ppermute(value, axis_name, pairs)
        step *= 2
    return value


def body(travel_time, crossing, bins, transmission, capture):
    tiles = lax.axis_size("tile")
    freqs = lax.axis_size("freq")
    k = lax.axis_index("tile")
    f = lax.axis_index("freq")

    positions = tiles // 2
    z = k // 2
    y = k % 2
    swap = [(j, j ^ 1) for j in range(tiles)]

    cap_row = [capture[0]]
    for s in range(1, positions):
        pairs = [(p * 2 + r, ((p - s) % positions) * 2 + r) for p in range(positions) for r in range(2)]
        cap_row.append(lax.ppermute(capture[0], "tile", pairs))
    own_swapped = lax.ppermute(capture[0], "tile", swap)

    per_tile = travel_time.shape[1] // tiles
    pieces = [lax.dynamic_slice_in_dim(travel_time, 2 * z * per_tile, 2 * per_tile, 1)]
    for s in range(1, positions):
        target = (z - s) % positions
        sent = lax.dynamic_slice_in_dim(travel_time, 2 * target * per_tile, 2 * per_tile, 1)
        pairs = [(p * 2 + r, ((p - s) % positions) * 2 + r) for p in range(positions) for r in range(2)]
        pieces.append(lax.ppermute(sent, "tile", pairs))
    pieces = jnp.stack(pieces)
    mine_tt = lax.dynamic_slice_in_dim(pieces, y * per_tile, per_tile, 2)
    theirs_tt = lax.ppermute(
        lax.dynamic_slice_in_dim(pieces, (1 - y) * per_tile, per_tile, 2), "tile", [(j, j ^ 1) for j in range(tiles)]
    )
    both_tt = jnp.stack([mine_tt, theirs_tt], axis=1)
    both_tt = jnp.roll(jnp.roll(both_tt, z, axis=0), y, axis=1)
    regrouped = both_tt.reshape((-1,) + both_tt.shape[3:])
    view = gather_columns(regrouped, "freq", freqs)
    view = jnp.moveaxis(view.reshape((freqs,) + regrouped.shape), 0, 2)
    elements, row_count, _, width = view.shape
    voxels = row_count * freqs * width

    turns = bins[0].astype(jnp.float32) * view.reshape(elements, voxels)
    angle = TWO_PI * (turns - jnp.round(turns))
    field_real = jnp.cos(angle).astype(jnp.bfloat16)
    field_imag = (-jnp.sin(angle)).astype(jnp.bfloat16)
    left = jnp.concatenate([field_real, field_imag], axis=1)
    right = jnp.concatenate([-field_imag, field_real], axis=1)

    row = cap_row
    other = (own_swapped, lax.ppermute(jnp.stack(row[1:]), "tile", swap))
    row = jnp.stack(row)
    own = capture.shape[2]

    def rows_of(field, which_row):
        grid = field.reshape(positions, 2, own, voxels)
        picked = lax.dynamic_index_in_dim(grid, which_row, 1, keepdims=False)
        return jnp.roll(picked, -z, axis=0).reshape(-1, voxels)

    def partial_focus(group, g_real, g_imag):
        cap_real = group[:, 0].reshape(-1, group.shape[-1])
        cap_imag = group[:, 1].reshape(-1, group.shape[-1])
        product = jnp.dot(cap_real, left, preferred_element_type=jnp.float32) + jnp.dot(
            cap_imag, right, preferred_element_type=jnp.float32
        )
        w_real = product[:, :voxels]
        w_imag = product[:, voxels:]
        g_real = g_real.astype(jnp.float32)
        g_imag = g_imag.astype(jnp.float32)
        part_real = jnp.sum(g_real * w_real - g_imag * w_imag, axis=0)
        part_imag = jnp.sum(g_real * w_imag + g_imag * w_real, axis=0)
        return part_real, part_imag

    mine_real, mine_imag = partial_focus(row, rows_of(field_real, y), rows_of(field_imag, y))
    theirs_rows = (rows_of(field_real, 1 - y), rows_of(field_imag, 1 - y))
    mine_real, mine_imag, theirs_rows, other = lax.optimization_barrier((mine_real, mine_imag, theirs_rows, other))
    theirs_real, theirs_imag = partial_focus(jnp.concatenate([other[0][None], other[1]]), *theirs_rows)
    focus_real = mine_real + theirs_real
    focus_imag = mine_imag + theirs_imag

    outer = freqs // 2
    focus = jnp.stack([focus_real, focus_imag]).reshape(2, row_count, outer, 2, width)
    focus = jnp.roll(focus, f % 2, axis=3)
    focus = jnp.roll(focus, f // 2, axis=2).reshape(2, row_count, freqs * width)
    focus_real = focus[0]
    focus_imag = focus[1]

    cells = transmission.shape[2]
    match = crossing[None] == lax.broadcasted_iota(jnp.int32, (cells, 1, 1), 0)
    coeff_real = jnp.sum(jnp.where(match, transmission[0, 0][:, None, None], jnp.float32(0.0)), axis=0)
    coeff_imag = jnp.sum(jnp.where(match, transmission[0, 1][:, None, None], jnp.float32(0.0)), axis=0)
    square_real = coeff_real * coeff_real - coeff_imag * coeff_imag
    square_imag = 2.0 * coeff_real * coeff_imag
    part_real = square_real * focus_real - square_imag * focus_imag
    part_imag = square_real * focus_imag + square_imag * focus_real
    partial_image = jnp.stack([part_real, part_imag])
    return all_sum_once(partial_image, "freq", freqs)


def solution(mesh):
    in_specs = (
        P("tile", None, "freq"),
        P("tile", None),
        P("freq"),
        P("freq", None, None),
        P("freq", None, "tile", None),
    )
    out_specs = P(None, "tile", None)
    return jax.shard_map(body, mesh=mesh, in_specs=in_specs, out_specs=out_specs, check_vma=False)
```

```python
import math

import jax
import jax.numpy as jnp
from jax import lax
from jax.sharding import PartitionSpec as P

TWO_PI = 2.0 * math.pi


def gather_shifted(block, axis_name, size):
    pieces = [block]
    for s in range(1, size):
        pairs = [(i, (i - s) % size) for i in range(size)]
        pieces.append(lax.ppermute(block, axis_name, pairs))
    return pieces


def chain(block, axis_name, size, stride, step, direction):
    positions = size // stride
    pairs = []
    for z in range(positions):
        target = z + direction
        if 0 <= target < positions and 0 <= z - direction * (step - 1) < positions:
            pairs += [(z * stride + y, target * stride + y) for y in range(stride)]
    return lax.ppermute(block, axis_name, pairs)


def line_gather(block, axis_name, size):
    positions = size // 2
    z = lax.axis_index(axis_name) // 2
    left = [block]
    right = [block]
    for j in range(1, positions):
        left.append(chain(left[-1], axis_name, size, 2, j, 1))
        right.append(chain(right[-1], axis_name, size, 2, j, -1))
    slots = left[:0:-1] + [block] + right[1:]
    return slots, z


def pair_swap(slots, axis_name, size):
    positions = size // 2
    centre = positions - 1
    out = []
    for i, piece in enumerate(slots):
        d = i - centre
        pairs = [(p * 2 + y, p * 2 + 1 - y) for p in range(positions) if 0 <= p + d < positions for y in range(2)]
        out.append(lax.ppermute(piece, axis_name, pairs))
    return out


def gather_rows(block, axis_name, size):
    positions = size // 2
    slots, z = line_gather(block, axis_name, size)
    other = pair_swap(slots, axis_name, size)
    mine = lax.dynamic_slice_in_dim(jnp.stack(slots), positions - 1 - z, positions, 0)
    theirs = lax.dynamic_slice_in_dim(jnp.stack(other), positions - 1 - z, positions, 0)
    both = jnp.stack([mine, theirs], axis=1)
    both = jnp.roll(both, lax.axis_index(axis_name) % 2, axis=1)
    return both.reshape((size,) + block.shape)


def gather_columns(block, axis_name, size):
    outer = size // 2
    same_core = [block]
    for s in range(1, outer):
        pairs = [(i, (i - 2 * s) % size) for i in range(size)]
        same_core.append(lax.ppermute(block, axis_name, pairs))
    swap = [(i, i ^ 1) for i in range(size)]
    partner = [lax.ppermute(piece, axis_name, swap) for piece in same_core]
    return jnp.stack([jnp.stack(same_core), jnp.stack(partner)], axis=1)


def gather_row_blocks(block, axis_name, size):
    positions = size // 2
    i = lax.axis_index(axis_name)
    z = i // 2
    y = i % 2
    row = [block]
    for s in range(1, positions):
        pairs = [(p * 2 + r, ((p - s) % positions) * 2 + r) for p in range(positions) for r in range(2)]
        row.append(lax.ppermute(block, axis_name, pairs))
    other = lax.ppermute(jnp.stack(row), axis_name, [(j, j ^ 1) for j in range(size)])
    out = []
    for s in range(positions):
        out.append((((z + s) % positions) * 2 + y, row[s]))
        out.append((((z + s) % positions) * 2 + 1 - y, other[s]))
    return out


def all_sum_once(value, axis_name, size):
    pieces = gather_shifted(value, axis_name, size)
    stacked = jnp.roll(jnp.stack(pieces), lax.axis_index(axis_name), axis=0)
    total = stacked[0]
    for j in range(1, size):
        total = total + stacked[j]
    return total


def all_sum(value, axis_name, size):
    step = 1
    while step < size:
        pairs = [(i, i ^ step) for i in range(size)]
        value = value + lax.ppermute(value, axis_name, pairs)
        step *= 2
    return value


def body(travel_time, crossing, bins, transmission, capture):
    tiles = lax.axis_size("tile")
    freqs = lax.axis_size("freq")
    k = lax.axis_index("tile")
    f = lax.axis_index("freq")

    positions = tiles // 2
    z = k // 2
    y = k % 2
    swap = [(j, j ^ 1) for j in range(tiles)]

    cap_row = [capture[0]]
    for s in range(1, positions):
        pairs = [(p * 2 + r, ((p - s) % positions) * 2 + r) for p in range(positions) for r in range(2)]
        cap_row.append(lax.ppermute(capture[0], "tile", pairs))
    own_swapped = lax.ppermute(capture[0], "tile", swap)

    per_tile = travel_time.shape[1] // tiles
    pieces = [lax.dynamic_slice_in_dim(travel_time, 2 * z * per_tile, 2 * per_tile, 1)]
    for s in range(1, positions):
        target = (z - s) % positions
        sent = lax.dynamic_slice_in_dim(travel_time, 2 * target * per_tile, 2 * per_tile, 1)
        pairs = [(p * 2 + r, ((p - s) % positions) * 2 + r) for p in range(positions) for r in range(2)]
        pieces.append(lax.ppermute(sent, "tile", pairs))
    pieces = jnp.stack(pieces)
    mine_tt = lax.dynamic_slice_in_dim(pieces, y * per_tile, per_tile, 2)
    theirs_tt = lax.ppermute(
        lax.dynamic_slice_in_dim(pieces, (1 - y) * per_tile, per_tile, 2), "tile", [(j, j ^ 1) for j in range(tiles)]
    )
    both_tt = jnp.stack([mine_tt, theirs_tt], axis=1)
    both_tt = jnp.roll(jnp.roll(both_tt, z, axis=0), y, axis=1)
    regrouped = both_tt.reshape((-1,) + both_tt.shape[3:])
    view = gather_columns(regrouped, "freq", freqs)
    view = jnp.moveaxis(view.reshape((freqs,) + regrouped.shape), 0, 2)
    elements, row_count, _, width = view.shape
    voxels = row_count * freqs * width

    scaled = TWO_PI * bins[0].astype(jnp.float32)
    angle = scaled * view.reshape(elements, voxels)
    field_real = jnp.cos(angle).astype(jnp.bfloat16)
    field_imag = (-jnp.sin(angle)).astype(jnp.bfloat16)
    left = jnp.concatenate([field_real, field_imag], axis=1)
    right = jnp.concatenate([-field_imag, field_real], axis=1)

    row = cap_row
    other = (own_swapped, lax.ppermute(jnp.stack(row[1:]), "tile", swap))
    row = jnp.stack(row)
    own = capture.shape[2]

    def rows_of(field, which_row):
        grid = field.reshape(positions, 2, own, voxels)
        picked = lax.dynamic_index_in_dim(grid, which_row, 1, keepdims=False)
        return jnp.roll(picked, -z, axis=0).reshape(-1, voxels)

    def partial_focus(group, g_real, g_imag):
        cap_real = group[:, 0].reshape(-1, group.shape[-1])
        cap_imag = group[:, 1].reshape(-1, group.shape[-1])
        product = jnp.dot(cap_real, left, preferred_element_type=jnp.float32) + jnp.dot(
            cap_imag, right, preferred_element_type=jnp.float32
        )
        w_real = product[:, :voxels]
        w_imag = product[:, voxels:]
        g_real = g_real.astype(jnp.float32)
        g_imag = g_imag.astype(jnp.float32)
        part_real = jnp.sum(g_real * w_real - g_imag * w_imag, axis=0)
        part_imag = jnp.sum(g_real * w_imag + g_imag * w_real, axis=0)
        return part_real, part_imag

    mine_real, mine_imag = partial_focus(row, rows_of(field_real, y), rows_of(field_imag, y))
    theirs_real_rows = rows_of(field_real, 1 - y)
    theirs_imag_rows = rows_of(field_imag, 1 - y)
    first_real, first_imag = partial_focus(other[0][None], theirs_real_rows[:own], theirs_imag_rows[:own])
    theirs_rows = (theirs_real_rows[own:], theirs_imag_rows[own:])
    mine_real, mine_imag, first_real, first_imag, theirs_rows, rest = lax.optimization_barrier(
        (mine_real, mine_imag, first_real, first_imag, theirs_rows, other[1])
    )
    theirs_real, theirs_imag = partial_focus(rest, *theirs_rows)
    focus_real = mine_real + (first_real + theirs_real)
    focus_imag = mine_imag + (first_imag + theirs_imag)

    outer = freqs // 2
    focus = jnp.stack([focus_real, focus_imag]).reshape(2, row_count, outer, 2, width)
    focus = jnp.roll(focus, f % 2, axis=3)
    focus = jnp.roll(focus, f // 2, axis=2).reshape(2, row_count, freqs * width)
    focus_real = focus[0]
    focus_imag = focus[1]

    cells = transmission.shape[2]
    match = crossing[None] == lax.broadcasted_iota(jnp.int32, (cells, 1, 1), 0)
    coeff_real = jnp.sum(jnp.where(match, transmission[0, 0][:, None, None], jnp.float32(0.0)), axis=0)
    coeff_imag = jnp.sum(jnp.where(match, transmission[0, 1][:, None, None], jnp.float32(0.0)), axis=0)
    square_real = coeff_real * coeff_real - coeff_imag * coeff_imag
    square_imag = 2.0 * coeff_real * coeff_imag
    part_real = square_real * focus_real - square_imag * focus_imag
    part_imag = square_real * focus_imag + square_imag * focus_real
    partial_image = jnp.stack([part_real, part_imag])
    return all_sum_once(partial_image, "freq", freqs)


def solution(mesh):
    in_specs = (
        P("tile", None, "freq"),
        P("tile", None),
        P("freq"),
        P("freq", None, None),
        P("freq", None, "tile", None),
    )
    out_specs = P(None, "tile", None)
    return jax.shard_map(body, mesh=mesh, in_specs=in_specs, out_specs=out_specs, check_vma=False)
```

```python
import math

import jax
import jax.numpy as jnp
from jax import lax
from jax.sharding import PartitionSpec as P

TWO_PI = 2.0 * math.pi


def gather_shifted(block, axis_name, size):
    pieces = [block]
    for s in range(1, size):
        pairs = [(i, (i - s) % size) for i in range(size)]
        pieces.append(lax.ppermute(block, axis_name, pairs))
    return pieces


def chain(block, axis_name, size, stride, step, direction):
    positions = size // stride
    pairs = []
    for z in range(positions):
        target = z + direction
        if 0 <= target < positions and 0 <= z - direction * (step - 1) < positions:
            pairs += [(z * stride + y, target * stride + y) for y in range(stride)]
    return lax.ppermute(block, axis_name, pairs)


def line_gather(block, axis_name, size):
    positions = size // 2
    z = lax.axis_index(axis_name) // 2
    left = [block]
    right = [block]
    for j in range(1, positions):
        left.append(chain(left[-1], axis_name, size, 2, j, 1))
        right.append(chain(right[-1], axis_name, size, 2, j, -1))
    slots = left[:0:-1] + [block] + right[1:]
    return slots, z


def pair_swap(slots, axis_name, size):
    positions = size // 2
    centre = positions - 1
    out = []
    for i, piece in enumerate(slots):
        d = i - centre
        pairs = [(p * 2 + y, p * 2 + 1 - y) for p in range(positions) if 0 <= p + d < positions for y in range(2)]
        out.append(lax.ppermute(piece, axis_name, pairs))
    return out


def gather_rows(block, axis_name, size):
    positions = size // 2
    slots, z = line_gather(block, axis_name, size)
    other = pair_swap(slots, axis_name, size)
    mine = lax.dynamic_slice_in_dim(jnp.stack(slots), positions - 1 - z, positions, 0)
    theirs = lax.dynamic_slice_in_dim(jnp.stack(other), positions - 1 - z, positions, 0)
    both = jnp.stack([mine, theirs], axis=1)
    both = jnp.roll(both, lax.axis_index(axis_name) % 2, axis=1)
    return both.reshape((size,) + block.shape)


def gather_columns(block, axis_name, size):
    outer = size // 2
    same_core = [block]
    for s in range(1, outer):
        pairs = [(i, (i - 2 * s) % size) for i in range(size)]
        same_core.append(lax.ppermute(block, axis_name, pairs))
    swap = [(i, i ^ 1) for i in range(size)]
    partner = [lax.ppermute(piece, axis_name, swap) for piece in same_core]
    return jnp.stack([jnp.stack(same_core), jnp.stack(partner)], axis=1)


def gather_row_blocks(block, axis_name, size):
    positions = size // 2
    i = lax.axis_index(axis_name)
    z = i // 2
    y = i % 2
    row = [block]
    for s in range(1, positions):
        pairs = [(p * 2 + r, ((p - s) % positions) * 2 + r) for p in range(positions) for r in range(2)]
        row.append(lax.ppermute(block, axis_name, pairs))
    other = lax.ppermute(jnp.stack(row), axis_name, [(j, j ^ 1) for j in range(size)])
    out = []
    for s in range(positions):
        out.append((((z + s) % positions) * 2 + y, row[s]))
        out.append((((z + s) % positions) * 2 + 1 - y, other[s]))
    return out


def all_sum_once(value, axis_name, size):
    pieces = gather_shifted(value, axis_name, size)
    stacked = jnp.roll(jnp.stack(pieces), lax.axis_index(axis_name), axis=0)
    total = stacked[0]
    for j in range(1, size):
        total = total + stacked[j]
    return total


def all_sum(value, axis_name, size):
    step = 1
    while step < size:
        pairs = [(i, i ^ step) for i in range(size)]
        value = value + lax.ppermute(value, axis_name, pairs)
        step *= 2
    return value


def body(travel_time, crossing, bins, transmission, capture):
    tiles = lax.axis_size("tile")
    freqs = lax.axis_size("freq")
    k = lax.axis_index("tile")
    f = lax.axis_index("freq")

    positions = tiles // 2
    z = k // 2
    y = k % 2
    swap = [(j, j ^ 1) for j in range(tiles)]

    cap_row = [capture[0]]
    for s in range(1, positions):
        pairs = [(p * 2 + r, ((p - s) % positions) * 2 + r) for p in range(positions) for r in range(2)]
        cap_row.append(lax.ppermute(capture[0], "tile", pairs))
    own_swapped = lax.ppermute(capture[0], "tile", swap)

    per_tile = travel_time.shape[1] // tiles
    pieces = [lax.dynamic_slice_in_dim(travel_time, 2 * z * per_tile, 2 * per_tile, 1)]
    for s in range(1, positions):
        target = (z - s) % positions
        sent = lax.dynamic_slice_in_dim(travel_time, 2 * target * per_tile, 2 * per_tile, 1)
        pairs = [(p * 2 + r, ((p - s) % positions) * 2 + r) for p in range(positions) for r in range(2)]
        pieces.append(lax.ppermute(sent, "tile", pairs))
    pieces = jnp.stack(pieces)
    mine_tt = lax.dynamic_slice_in_dim(pieces, y * per_tile, per_tile, 2)
    theirs_tt = lax.ppermute(
        lax.dynamic_slice_in_dim(pieces, (1 - y) * per_tile, per_tile, 2), "tile", [(j, j ^ 1) for j in range(tiles)]
    )
    both_tt = jnp.stack([mine_tt, theirs_tt], axis=1)
    both_tt = jnp.roll(jnp.roll(both_tt, z, axis=0), y, axis=1)
    regrouped = both_tt.reshape((-1,) + both_tt.shape[3:])
    view = gather_columns(regrouped, "freq", freqs)
    view = jnp.moveaxis(view.reshape((freqs,) + regrouped.shape), 0, 2)
    elements, row_count, _, width = view.shape
    voxels = row_count * freqs * width

    scaled = TWO_PI * bins[0].astype(jnp.float32)
    angle = scaled * view.reshape(elements, voxels)
    field_real = jnp.cos(angle).astype(jnp.bfloat16)
    field_imag = (-jnp.sin(angle)).astype(jnp.bfloat16)
    left = jnp.concatenate([field_real, field_imag], axis=1)
    right = jnp.concatenate([-field_imag, field_real], axis=1)

    row = cap_row
    other = (own_swapped, lax.ppermute(jnp.stack(row[1:]), "tile", swap))
    row = jnp.stack(row)
    own = capture.shape[2]

    def rows_of(field, which_row):
        grid = field.reshape(positions, 2, own, voxels)
        picked = lax.dynamic_index_in_dim(grid, which_row, 1, keepdims=False)
        return jnp.roll(picked, -z, axis=0).reshape(-1, voxels)

    def partial_focus(group, g_real, g_imag):
        cap_real = group[:, 0].reshape(-1, group.shape[-1])
        cap_imag = group[:, 1].reshape(-1, group.shape[-1])
        product = jnp.dot(cap_real, left, preferred_element_type=jnp.float32) + jnp.dot(
            cap_imag, right, preferred_element_type=jnp.float32
        )
        w_real = product[:, :voxels]
        w_imag = product[:, voxels:]
        g_real = g_real.astype(jnp.float32)
        g_imag = g_imag.astype(jnp.float32)
        part_real = jnp.sum(g_real * w_real - g_imag * w_imag, axis=0)
        part_imag = jnp.sum(g_real * w_imag + g_imag * w_real, axis=0)
        return part_real, part_imag

    mine_real, mine_imag = partial_focus(row, rows_of(field_real, y), rows_of(field_imag, y))
    theirs_rows = (rows_of(field_real, 1 - y), rows_of(field_imag, 1 - y))
    mine_real, mine_imag, theirs_rows, other = lax.optimization_barrier((mine_real, mine_imag, theirs_rows, other))
    theirs_real, theirs_imag = partial_focus(jnp.concatenate([other[0][None], other[1]]), *theirs_rows)
    focus_real = mine_real + theirs_real
    focus_imag = mine_imag + theirs_imag

    outer = freqs // 2
    focus = jnp.stack([focus_real, focus_imag]).reshape(2, row_count, outer, 2, width)
    focus = jnp.roll(focus, f % 2, axis=3)
    focus = jnp.roll(focus, f // 2, axis=2).reshape(2, row_count, freqs * width)
    focus_real = focus[0]
    focus_imag = focus[1]

    cells = transmission.shape[2]
    match = crossing[None] == lax.broadcasted_iota(jnp.int32, (cells, 1, 1), 0)
    coeff_real = jnp.sum(jnp.where(match, transmission[0, 0][:, None, None], jnp.float32(0.0)), axis=0)
    coeff_imag = jnp.sum(jnp.where(match, transmission[0, 1][:, None, None], jnp.float32(0.0)), axis=0)
    square_real = coeff_real * coeff_real - coeff_imag * coeff_imag
    square_imag = 2.0 * coeff_real * coeff_imag
    part_real = square_real * focus_real - square_imag * focus_imag
    part_imag = square_real * focus_imag + square_imag * focus_real
    partial_image = jnp.stack([part_real, part_imag])
    return all_sum(partial_image, "freq", freqs)


def solution(mesh):
    in_specs = (
        P("tile", None, "freq"),
        P("tile", None),
        P("freq"),
        P("freq", None, None),
        P("freq", None, "tile", None),
    )
    out_specs = P(None, "tile", None)
    return jax.shard_map(body, mesh=mesh, in_specs=in_specs, out_specs=out_specs, check_vma=False)
```
